256 devices in a mesh: segment: 2 (over y_hi), blk: 32 (over z, x), mp: 4 (over y_lo, core).
Axes of the slice: x: 4, y: 4 (y_hi: 2, y_lo: 2; y = y_hi * 2 + y_lo), z: 8, core: 2. Of those that a mesh axis runs over, the one named last changes fastest.
Arguments:
- section_input: bfloat16 [2, 8192, 1536], P('segment', 'blk', 'mp'), may hold values from -36 to 36
- row_code: int32 [2, 8192], P('segment', 'blk'), may hold values from 0 to 255
- code_table: bfloat16 [2, 256, 1536], P('segment', None, 'mp'), may hold values from -6 to 6
- self_gain: float32 [2, 1536], P('segment'), may hold values from 0.1 to 1.9
- self_weights: bfloat16 [2, 3, 1536, 1536], P('segment', None, None, 'mp'), may hold values from -0.22963966 to 0.22963966
- self_out: bfloat16 [2, 1536, 1536], P('segment', 'mp'), may hold values from -0.15625 to 0.15625
- cross_gain: float32 [1536], replicated, may hold values from 0.1 to 1.9
- memory_gain: float32 [1536], replicated, may hold values from 0.1 to 1.9
- cross_weights: bfloat16 [3, 1536, 1536], P(None, None, 'mp'), may hold values from -0.22963966 to 0.22963966
- cross_out: bfloat16 [1536, 1536], P('mp'), may hold values from -0.15625 to 0.15625
Outputs:
- sections: bfloat16 [2, 8192, 1536], P('segment', 'blk', 'mp')
The draws below stay inside these ranges and needn't reach their ends.
All inputs are finite; a program needn't handle non-finite values.
Results may differ from the reference program's by a relative error of at most 0.0085.
Values may be sent and summed in bfloat16 or wider, within the bound.
No kernel may reach another device: no remote copies, remote signals or barrier semaphores. Data moves between devices by JAX's collectives and lax.ppermute only.
A program may use at most 128 MiB of HBM per device.

```python
import math
import jax
import jax.numpy as jnp
from jax import lax

D = 1536
HEAD_DIM = 128
CODES = 256
NT = 8192


def projection_draw(key, salt, leading):
    shape = leading + (3, D, D)
    base = jnp.clip(jax.random.normal(jax.random.fold_in(key, salt), shape, jnp.float32), -6.0, 6.0)
    factors = jnp.array([math.sqrt(2.0 / D), math.sqrt(2.0 / D), math.sqrt(1.0 / D)], jnp.float32)
    values = base * factors[:, None, None]
    return values.astype(jnp.bfloat16)


def draw_section_input(key, part):
    noise = jnp.clip(jax.random.normal(jax.random.fold_in(key, 11), (2, NT, D), jnp.float32), -5.0, 5.0)
    values = noise
    return values.astype(jnp.bfloat16)


def draw_self_weights(key, part):
    return projection_draw(key, 21, (2,))


def draw_cross_weights(key, part):
    return projection_draw(key, 31, ())


def touch_ends(values, rng, smallest, high):
    spot = [jax.random.randint(jax.random.fold_in(rng, axis), (), 0, length) for axis, length in enumerate(values.shape)]
    widest = values.shape.index(max(values.shape))
    neighbour = spot[:widest] + [(spot[widest] + 1) % values.shape[widest]] + spot[widest + 1:]
    return values.at[tuple(spot)].set(smallest).at[tuple(neighbour)].set(high)


def shard_levels(stream_key, dims, split, low, high):
    level, own = 1.0, jax.random.fold_in(stream_key, 6)
    for position, parts in split:
        heights = jnp.exp(jax.random.uniform(jax.random.fold_in(own, position), (parts,), jnp.float32, low / len(split), high / len(split)))
        level = level * jnp.repeat(heights, dims[position] // parts).reshape([-1 if axis == position else 1 for axis in range(len(dims))])
    return level


def normal_values(key, extent, deviation, most, split=(), held_as=jnp.bfloat16):
    level = shard_levels(key, extent, split, -0.22, 0.18) if split else 1.0
    values = jax.random.normal(key, extent, jnp.float32) * deviation * level
    return jnp.minimum(jnp.maximum(values, -most), most).astype(held_as)


def setup_inputs(seed: int = 0) -> dict:
    streams_of = jax.random.split(jax.random.key(seed), 11)
    section_input = draw_section_input(jax.random.fold_in(streams_of[10], 71), 0)
    row_code = touch_ends(jax.random.randint(streams_of[1], (2, NT), 0, CODES), jax.random.fold_in(streams_of[1], 1), 0, CODES - 1).astype(jnp.int32)
    code_table = normal_values(streams_of[2], (2, CODES, D), 1.0, 6.0, ((0, 2), (2, 4)))
    self_gain = jnp.clip(1.0 + 0.18 * jax.random.normal(streams_of[3], (2, D), jnp.float32), 0.1, 1.9)
    self_weights = draw_self_weights(jax.random.fold_in(streams_of[10], 71), 0)
    self_out = normal_values(streams_of[5], (2, D, D), D ** -0.5, 0.15625, ((0, 2), (1, 4)))
    cross_gain = jnp.clip(1.0 + 0.18 * jax.random.normal(streams_of[6], (D,), jnp.float32), 0.1, 1.9)
    memory_gain = jnp.clip(1.0 + 0.18 * jax.random.normal(streams_of[7], (D,), jnp.float32), 0.1, 1.9)
    cross_weights = draw_cross_weights(jax.random.fold_in(streams_of[10], 71), 0)
    cross_out = normal_values(streams_of[9], (D, D), D ** -0.5, 0.15625, ((0, 4),))
    return {"section_input": section_input, "row_code": row_code, "code_table": code_table, "self_gain": self_gain, "self_weights": self_weights, "self_out": self_out, "cross_gain": cross_gain, "memory_gain": memory_gain, "cross_weights": cross_weights, "cross_out": cross_out}


def rms_norm(values, gain):
    widened = values.astype(jnp.float32)
    meansq = lax.optimization_barrier(jnp.mean(widened * widened, axis=-1, keepdims=True))
    return (widened * lax.rsqrt(meansq + 1e-05) * gain).astype(jnp.bfloat16)

def attention(queries, keys, values):
    row_count = queries.shape[0]
    head_count = queries.shape[1] // HEAD_DIM
    query_heads = queries.reshape(row_count, head_count, HEAD_DIM).transpose(1, 0, 2)
    key_heads = keys.reshape(keys.shape[0], head_count, HEAD_DIM).transpose(1, 0, 2)
    value_heads = values.reshape(values.shape[0], head_count, HEAD_DIM).transpose(1, 0, 2)

    def one_head(operands):
        query_one, key_one, value_one = operands
        scores = jnp.dot(query_one, key_one.T, preferred_element_type=jnp.float32) * (1.0 / math.sqrt(HEAD_DIM))
        largest = lax.optimization_barrier(jnp.max(scores, axis=1, keepdims=True))
        weights = jnp.exp(scores - largest)
        summed = lax.optimization_barrier(jnp.sum(weights, axis=1, keepdims=True))
        result = jnp.dot(weights.astype(jnp.bfloat16), value_one, preferred_element_type=jnp.float32) / summed
        return result.astype(jnp.bfloat16)
    outputs = lax.map(one_head, (query_heads, key_heads, value_heads))
    return outputs.transpose(1, 0, 2).reshape(row_count, head_count * HEAD_DIM)

def section(inputs, codes, table, gain, weights, out_weight):
    looked = jnp.take(table, codes, axis=0)
    embedded = (inputs.astype(jnp.float32) + looked.astype(jnp.float32)).astype(jnp.bfloat16)
    normed = rms_norm(embedded, gain)
    queries = jnp.dot(normed, weights[0], preferred_element_type=jnp.float32).astype(jnp.bfloat16)
    keys = jnp.dot(normed, weights[1], preferred_element_type=jnp.float32).astype(jnp.bfloat16)
    values = jnp.dot(normed, weights[2], preferred_element_type=jnp.float32).astype(jnp.bfloat16)
    attended = attention(queries, keys, values)
    return (embedded.astype(jnp.float32) + jnp.dot(attended, out_weight, preferred_element_type=jnp.float32)).astype(jnp.bfloat16)

def reference(section_input, row_code, code_table, self_gain, self_weights, self_out, cross_gain, memory_gain, cross_weights, cross_out):
    memory = section(section_input[0], row_code[0], code_table[0], self_gain[0], self_weights[0], self_out[0])
    voxel = section(section_input[1], row_code[1], code_table[1], self_gain[1], self_weights[1], self_out[1])
    memory_normed = rms_norm(memory, memory_gain)
    cross_keys = jnp.dot(memory_normed, cross_weights[1], preferred_element_type=jnp.float32).astype(jnp.bfloat16)
    cross_values = jnp.dot(memory_normed, cross_weights[2], preferred_element_type=jnp.float32).astype(jnp.bfloat16)
    cross_queries = jnp.dot(rms_norm(voxel, cross_gain), cross_weights[0], preferred_element_type=jnp.float32).astype(jnp.bfloat16)
    cross_attended = attention(cross_queries, cross_keys, cross_values)
    decoded = (voxel.astype(jnp.float32) + jnp.dot(cross_attended, cross_out, preferred_element_type=jnp.float32)).astype(jnp.bfloat16)
    return jnp.stack([memory, decoded])
```

```python
import math

import jax
import jax.numpy as jnp
from jax import lax
from jax.sharding import PartitionSpec as P
from jax.experimental import pallas as pl
from jax.experimental.pallas import tpu as pltpu

HEAD_DIM = 128


def shifted(value, axis, steps):
    count = lax.axis_size(axis)
    initial, last = (max(0, -steps), min(count, count - steps))
    return lax.ppermute(value, axis, [(source, source + steps) for source in range(initial, last)])


def rms_norm(values, gain):
    widened = values.astype(jnp.float32)
    meansq = jnp.mean(widened * widened, axis=-1, keepdims=True)
    return (widened * lax.rsqrt(meansq + 1e-05) * gain).astype(jnp.bfloat16)


def project(normed, weight):
    return jnp.dot(normed, weight, preferred_element_type=jnp.float32).astype(jnp.bfloat16)


def make_fold(queries):
    row_count = queries.shape[0]
    head_count = queries.shape[1] // HEAD_DIM
    grouped = queries.reshape(row_count, head_count, HEAD_DIM)
    factor = 1.0 / math.sqrt(HEAD_DIM)

    def fold(running, piece, start):
        piece_rows = piece.shape[1]
        block_rows = math.gcd(piece_rows, 1024)
        key_blocks = piece[0].reshape(piece_rows // block_rows, block_rows, head_count, HEAD_DIM)
        value_blocks = piece[1].reshape(piece_rows // block_rows, block_rows, head_count, HEAD_DIM)

        def absorb(current, blocks):
            running_max, running_sum, running_out = current
            key_block, value_block = blocks
            scores = (
                jnp.einsum("qhd,khd->qhk", grouped, key_block, preferred_element_type=jnp.float32)
                * factor
            )
            new_max = jnp.maximum(running_max, jnp.max(scores, axis=2))
            shrink = jnp.exp(running_max - new_max)
            weights = jnp.exp(scores - new_max[:, :, None])
            new_sum = running_sum * shrink + jnp.sum(weights, axis=2)
            new_out = running_out * shrink[:, :, None] + jnp.einsum(
                "qhk,khd->qhd",
                weights.astype(jnp.bfloat16),
                value_block,
                preferred_element_type=jnp.float32,
            )
            return ((new_max, new_sum, new_out), None)

        result, unused = lax.scan(absorb, running, (key_blocks, value_blocks))
        return result

    start_state = (
        jnp.full((row_count, head_count), -1e30, jnp.float32),
        jnp.zeros((row_count, head_count), jnp.float32),
        jnp.zeros((row_count, head_count, HEAD_DIM), jnp.float32),
    )
    return (fold, start_state)


def finish(running):
    running_max, running_sum, running_out = running
    merged = running_out / running_sum[:, :, None]
    return merged.reshape(merged.shape[0], merged.shape[1] * merged.shape[2]).astype(jnp.bfloat16)


def attend_kernel(q_ref, k_ref, v_ref, o_ref):
    scores = lax.dot_general(
        q_ref[...], k_ref[...], (((1,), (1,)), ((), ())), preferred_element_type=jnp.float32
    ) * (1.0 / math.sqrt(HEAD_DIM))
    largest = jnp.max(scores, axis=1, keepdims=True)
    weights = jnp.exp(scores - largest)
    summed = jnp.sum(weights, axis=1, keepdims=True)
    result = jnp.dot(weights.astype(jnp.bfloat16), v_ref[...], preferred_element_type=jnp.float32)
    o_ref[...] = (result / summed).astype(o_ref.dtype)


def attend(queries, pairs):
    rows, width = queries.shape
    keys = pairs.shape[1]
    heads = width // HEAD_DIM
    return pl.pallas_call(
        attend_kernel,
        grid=(heads,),
        in_specs=[
            pl.BlockSpec((rows, HEAD_DIM), lambda h: (0, h)),
            pl.BlockSpec((None, keys, HEAD_DIM), lambda h: (0, 0, h)),
            pl.BlockSpec((None, keys, HEAD_DIM), lambda h: (1, 0, h)),
        ],
        out_specs=pl.BlockSpec((rows, HEAD_DIM), lambda h: (0, h)),
        out_shape=jax.ShapeDtypeStruct((rows, width), jnp.bfloat16),
        compiler_params=pltpu.CompilerParams(vmem_limit_bytes=48 * 1024 * 1024),
    )(queries, pairs, pairs)


def memory_projection(memory_full, memory_gain, cross_weights):
    memory_normed = rms_norm(memory_full, memory_gain)
    return jnp.stack(
        [project(memory_normed, cross_weights[1]), project(memory_normed, cross_weights[2])]
    )


def on_device(
    section_input,
    row_code,
    code_table,
    self_gain,
    self_weights,
    self_out,
    cross_gain,
    memory_gain,
    cross_weights,
    cross_out,
):
    local_rows = section_input.shape[1]
    codes_total = code_table.shape[1]
    matches = (
        row_code[0][:, None] == lax.broadcasted_iota(jnp.int32, (local_rows, codes_total), 1)
    ).astype(jnp.bfloat16)
    looked = jnp.dot(matches, code_table[0], preferred_element_type=jnp.float32)
    embedded = (section_input[0].astype(jnp.float32) + looked).astype(jnp.bfloat16)
    embedded_full = lax.all_gather(embedded, "mp", axis=1, tiled=True)
    normed = rms_norm(embedded_full, self_gain[0])
    self_queries = project(normed, self_weights[0, 0])
    self_pairs = jnp.stack(
        [project(normed, self_weights[0, 1]), project(normed, self_weights[0, 2])]
    )
    self_attended = attend(self_queries, lax.all_gather(self_pairs, "blk", axis=1, tiled=True))
    partial_out = jnp.dot(self_attended, self_out[0], preferred_element_type=jnp.float32)
    reduced = lax.psum_scatter(
        partial_out.astype(jnp.bfloat16), "mp", scatter_dimension=1, tiled=True
    ).astype(jnp.float32)
    hidden_part = (embedded.astype(jnp.float32) + reduced).astype(jnp.bfloat16)
    hidden_full = lax.all_gather(hidden_part, "mp", axis=1, tiled=True)
    cross_queries = project(rms_norm(hidden_full, cross_gain), cross_weights[0])
    arrived = shifted(hidden_part, "segment", 1)
    memory_full = lax.all_gather(arrived, "mp", axis=1, tiled=True)
    memory_pairs = memory_projection(memory_full, memory_gain, cross_weights)
    crossed = attend(cross_queries, lax.all_gather(memory_pairs, "blk", axis=1, tiled=True))
    cross_partial = jnp.dot(crossed, cross_out, preferred_element_type=jnp.float32)
    cross_reduced = lax.psum_scatter(
        cross_partial.astype(jnp.bfloat16), "mp", scatter_dimension=1, tiled=True
    ).astype(jnp.float32)
    decoded = (hidden_part.astype(jnp.float32) + cross_reduced).astype(jnp.bfloat16)
    chosen = jnp.where(lax.axis_index("segment") == 0, hidden_part, decoded)
    return chosen[None]


def solution(mesh):
    return jax.shard_map(
        on_device,
        mesh=mesh,
        in_specs=(
            P("segment", "blk", "mp"),
            P("segment", "blk"),
            P("segment", None, "mp"),
            P("segment", None),
            P("segment", None, None, "mp"),
            P("segment", "mp", None),
            P(),
            P(),
            P(None, None, "mp"),
            P("mp", None),
        ),
        out_specs=P("segment", "blk", "mp"),
        check_vma=False,
    )
```

```python
import math

import jax
import jax.numpy as jnp
from jax import lax
from jax.experimental import pallas as pl
from jax.experimental.pallas import tpu as pltpu
from jax.sharding import Mesh
from jax.sharding import PartitionSpec as P

HEAD_DIM = 128
X_SIZE = 4
TILE = 256
STATS = 128


def shifted(value, axis, steps):
    count = lax.axis_size(axis)
    initial, last = (max(0, -steps), min(count, count - steps))
    return lax.ppermute(value, axis, [(source, source + steps) for source in range(initial, last)])


def rms_norm(values, gain):
    widened = values.astype(jnp.float32)
    meansq = jnp.mean(widened * widened, axis=-1, keepdims=True)
    return (widened * lax.rsqrt(meansq + 1e-05) * gain).astype(jnp.bfloat16)


def project(normed, weight):
    return jnp.dot(normed, weight, preferred_element_type=jnp.float32).astype(jnp.bfloat16)


def partial_kernel(q_ref, k_ref, v_ref, o_ref):
    heads = q_ref.shape[1] // HEAD_DIM
    rows = q_ref.shape[0]
    lane = lax.broadcasted_iota(jnp.int32, (rows, STATS), 1)
    stats = jnp.zeros((rows, STATS), jnp.float32)
    for h in range(heads):
        cols = slice(h * HEAD_DIM, (h + 1) * HEAD_DIM)
        scores = lax.dot_general(
            q_ref[:, cols], k_ref[:, cols], (((1,), (1,)), ((), ())),
            preferred_element_type=jnp.float32,
        ) * (1.0 / math.sqrt(HEAD_DIM))
        largest = jnp.max(scores, axis=1, keepdims=True)
        weights = jnp.exp(scores - largest)
        summed = jnp.sum(weights, axis=1, keepdims=True)
        o_ref[:, cols] = jnp.dot(
            weights.astype(jnp.bfloat16), v_ref[:, cols], preferred_element_type=jnp.float32
        )
        stats = jnp.where(lane == h, largest, stats)
        stats = jnp.where(lane == heads + h, summed, stats)
    o_ref[:, heads * HEAD_DIM:] = stats


def partial_attend(queries, pairs):
    rows, width = queries.shape
    keys = pairs.shape[1]
    return pl.pallas_call(
        partial_kernel,
        grid=(rows // TILE,),
        in_specs=[
            pl.BlockSpec((TILE, width), lambda i: (i, 0)),
            pl.BlockSpec((None, keys, width), lambda i: (0, 0, 0)),
            pl.BlockSpec((None, keys, width), lambda i: (1, 0, 0)),
        ],
        out_specs=pl.BlockSpec((TILE, width + STATS), lambda i: (i, 0)),
        out_shape=jax.ShapeDtypeStruct((rows, width + STATS), jnp.float32),
        compiler_params=pltpu.CompilerParams(vmem_limit_bytes=48 * 1024 * 1024),
    )(queries, pairs, pairs)


def attend(queries, pairs):
    rows, width = queries.shape
    heads = width // HEAD_DIM
    query_block = lax.all_gather(queries, "bx", axis=0, tiled=True)
    key_block = lax.all_gather(pairs, "bz", axis=1, tiled=True)
    partial = partial_attend(query_block, key_block)
    parts = lax.all_to_all(partial, "bx", 0, 0, tiled=True)
    parts = parts.reshape(-1, rows, width + STATS)
    outs = parts[:, :, :width].reshape(-1, rows, heads, HEAD_DIM)
    maxes = parts[:, :, width:width + heads]
    sums = parts[:, :, width + heads:width + 2 * heads]
    top = jnp.max(maxes, axis=0)
    scale = jnp.exp(maxes - top[None])
    total = jnp.sum(sums * scale, axis=0)
    merged = jnp.sum(outs * scale[..., None], axis=0) / total[..., None]
    return merged.reshape(rows, width).astype(jnp.bfloat16)


def memory_projection(memory_full, memory_gain, cross_weights):
    memory_normed = rms_norm(memory_full, memory_gain)
    return jnp.stack(
        [project(memory_normed, cross_weights[1]), project(memory_normed, cross_weights[2])]
    )


def on_device(
    section_input,
    row_code,
    code_table,
    self_gain,
    self_weights,
    self_out,
    cross_gain,
    memory_gain,
    cross_weights,
    cross_out,
):
    local_rows = section_input.shape[1]
    codes_total = code_table.shape[1]
    matches = (
        row_code[0][:, None] == lax.broadcasted_iota(jnp.int32, (local_rows, codes_total), 1)
    ).astype(jnp.bfloat16)
    looked = jnp.dot(matches, code_table[0], preferred_element_type=jnp.float32)
    embedded = (section_input[0].astype(jnp.float32) + looked).astype(jnp.bfloat16)
    embedded_full = lax.all_gather(embedded, "mp", axis=1, tiled=True)
    normed = rms_norm(embedded_full, self_gain[0])
    self_queries = project(normed, self_weights[0, 0])
    self_pairs = jnp.stack(
        [project(normed, self_weights[0, 1]), project(normed, self_weights[0, 2])]
    )
    self_attended = attend(self_queries, self_pairs)
    partial_out = jnp.dot(self_attended, self_out[0], preferred_element_type=jnp.float32)
    reduced = lax.psum_scatter(
        partial_out.astype(jnp.bfloat16), "mp", scatter_dimension=1, tiled=True
    ).astype(jnp.float32)
    hidden_part = (embedded.astype(jnp.float32) + reduced).astype(jnp.bfloat16)
    hidden_full = lax.all_gather(hidden_part, "mp", axis=1, tiled=True)
    cross_queries = project(rms_norm(hidden_full, cross_gain), cross_weights[0])
    arrived = shifted(hidden_part, "segment", 1)
    memory_full = lax.all_gather(arrived, "mp", axis=1, tiled=True)
    memory_pairs = memory_projection(memory_full, memory_gain, cross_weights)
    crossed = attend(cross_queries, memory_pairs)
    cross_partial = jnp.dot(crossed, cross_out, preferred_element_type=jnp.float32)
    cross_reduced = lax.psum_scatter(
        cross_partial.astype(jnp.bfloat16), "mp", scatter_dimension=1, tiled=True
    ).astype(jnp.float32)
    decoded = (hidden_part.astype(jnp.float32) + cross_reduced).astype(jnp.bfloat16)
    chosen = jnp.where(lax.axis_index("segment") == 0, hidden_part, decoded)
    return chosen[None]


def solution(mesh):
    segments, blocks, parts = (mesh.shape["segment"], mesh.shape["blk"], mesh.shape["mp"])
    split = Mesh(
        mesh.devices.reshape(segments, blocks // X_SIZE, X_SIZE, parts),
        ("segment", "bz", "bx", "mp"),
    )
    rows = ("bz", "bx")
    return jax.shard_map(
        on_device,
        mesh=split,
        in_specs=(
            P("segment", rows, "mp"),
            P("segment", rows),
            P("segment", None, "mp"),
            P("segment", None),
            P("segment", None, None, "mp"),
            P("segment", "mp", None),
            P(),
            P(),
            P(None, None, "mp"),
            P("mp", None),
        ),
        out_specs=P("segment", rows, "mp"),
        check_vma=False,
    )
```

```python
import math

import jax
import jax.numpy as jnp
from jax import lax
from jax.experimental import pallas as pl
from jax.experimental.pallas import tpu as pltpu
from jax.sharding import Mesh
from jax.sharding import PartitionSpec as P

HEAD_DIM = 128
X_SIZE = 4
TILE = 256
STATS = 128


def shifted(value, axis, steps):
    count = lax.axis_size(axis)
    initial, last = (max(0, -steps), min(count, count - steps))
    return lax.ppermute(value, axis, [(source, source + steps) for source in range(initial, last)])


def rms_norm(values, gain):
    widened = values.astype(jnp.float32)
    meansq = jnp.mean(widened * widened, axis=-1, keepdims=True)
    return (widened * lax.rsqrt(meansq + 1e-05) * gain).astype(jnp.bfloat16)


def project(normed, weight):
    return jnp.dot(normed, weight, preferred_element_type=jnp.float32).astype(jnp.bfloat16)


def partial_kernel(q_ref, k_ref, v_ref, o_ref):
    heads = q_ref.shape[1] // HEAD_DIM
    rows = q_ref.shape[0]
    lane = lax.broadcasted_iota(jnp.int32, (rows, STATS), 1)
    stats = jnp.zeros((rows, STATS), jnp.float32)
    for h in range(heads):
        cols = slice(h * HEAD_DIM, (h + 1) * HEAD_DIM)
        scores = lax.dot_general(
            q_ref[:, cols], k_ref[:, cols], (((1,), (1,)), ((), ())),
            preferred_element_type=jnp.float32,
        ) * (1.0 / math.sqrt(HEAD_DIM))
        largest = jnp.max(scores, axis=1, keepdims=True)
        weights = jnp.exp(scores - largest)
        summed = jnp.sum(weights, axis=1, keepdims=True)
        o_ref[:, cols] = jnp.dot(
            weights.astype(jnp.bfloat16), v_ref[:, cols], preferred_element_type=jnp.float32
        )
        stats = jnp.where(lane == h, largest, stats)
        stats = jnp.where(lane == heads + h, summed, stats)
    o_ref[:, heads * HEAD_DIM:] = stats


def partial_attend(queries, pairs):
    rows, width = queries.shape
    keys = pairs.shape[1]
    return pl.pallas_call(
        partial_kernel,
        grid=(rows // TILE,),
        in_specs=[
            pl.BlockSpec((TILE, width), lambda i: (i, 0)),
            pl.BlockSpec((None, keys, width), lambda i: (0, 0, 0)),
            pl.BlockSpec((None, keys, width), lambda i: (1, 0, 0)),
        ],
        out_specs=pl.BlockSpec((TILE, width + STATS), lambda i: (i, 0)),
        out_shape=jax.ShapeDtypeStruct((rows, width + STATS), jnp.float32),
        compiler_params=pltpu.CompilerParams(vmem_limit_bytes=48 * 1024 * 1024),
    )(queries, pairs, pairs)


def attend(queries, pairs, riders=None):
    rows, width = queries.shape
    heads = width // HEAD_DIM
    query_block = lax.all_gather(queries, "bx", axis=0, tiled=True)
    key_block = lax.all_gather(pairs, "bz", axis=1, tiled=True)
    if riders is not None:
        key_block, riders = lax.optimization_barrier((key_block, riders))
    partial = partial_attend(query_block, key_block)
    parts = lax.all_to_all(partial, "bx", 0, 0, tiled=True)
    parts = parts.reshape(-1, rows, width + STATS)
    outs = parts[:, :, :width].reshape(-1, rows, heads, HEAD_DIM)
    maxes = parts[:, :, width:width + heads]
    sums = parts[:, :, width + heads:width + 2 * heads]
    top = jnp.max(maxes, axis=0)
    scale = jnp.exp(maxes - top[None])
    total = jnp.sum(sums * scale, axis=0)
    merged = jnp.sum(outs * scale[..., None], axis=0) / total[..., None]
    merged = merged.reshape(rows, width).astype(jnp.bfloat16)
    return merged if riders is None else (merged, riders)


def spread(block_of):
    count = lax.axis_size("mp")
    me = lax.axis_index("mp")
    blocks = [(me, block_of(me))]
    for step in range(1, count):
        piece = block_of((me + step) % count)
        received = lax.ppermute(piece, "mp", [(j, (j + step) % count) for j in range(count)])
        blocks.append(((me - step + count) % count, received))
    return blocks


def project_out(attended_full, blocks):
    width = blocks[0][1].shape[0]
    total = None
    for source, block in blocks:
        piece = lax.dynamic_slice_in_dim(attended_full, source * width, width, axis=1)
        term = jnp.dot(piece, block, preferred_element_type=jnp.float32)
        total = term if total is None else total + term
    return total


def on_device(
    section_input,
    row_code,
    code_table,
    self_gain,
    self_weights,
    self_out,
    cross_gain,
    memory_gain,
    cross_weights,
    cross_out,
):
    local_rows = section_input.shape[1]
    local_width = section_input.shape[2]
    codes_total = code_table.shape[1]
    me = lax.axis_index("mp")
    self_blocks = spread(lambda target: self_out[0])
    cross_blocks = spread(
        lambda target: lax.dynamic_slice_in_dim(cross_out, target * local_width, local_width, axis=1)
    )
    matches = (
        row_code[0][:, None] == lax.broadcasted_iota(jnp.int32, (local_rows, codes_total), 1)
    ).astype(jnp.bfloat16)
    looked = jnp.dot(matches, code_table[0], preferred_element_type=jnp.float32)
    embedded = (section_input[0].astype(jnp.float32) + looked).astype(jnp.bfloat16)
    embedded_full = lax.all_gather(embedded, "mp", axis=1, tiled=True)
    normed = rms_norm(embedded_full, self_gain[0])
    self_queries = project(normed, self_weights[0, 0])
    self_pairs = jnp.stack(
        [project(normed, self_weights[0, 1]), project(normed, self_weights[0, 2])]
    )
    self_local, (self_blocks, cross_blocks) = attend(
        self_queries, self_pairs, (self_blocks, cross_blocks)
    )
    self_attended = lax.all_gather(self_local, "mp", axis=1, tiled=True)
    hidden_full = (
        embedded_full.astype(jnp.float32) + project_out(self_attended, self_blocks)
    ).astype(jnp.bfloat16)
    hidden_part = lax.dynamic_slice_in_dim(hidden_full, me * local_width, local_width, axis=1)
    cross_queries = project(rms_norm(hidden_full, cross_gain), cross_weights[0])
    memory_normed = rms_norm(hidden_full, memory_gain)
    memory_pairs = jnp.stack(
        [project(memory_normed, cross_weights[1]), project(memory_normed, cross_weights[2])]
    )
    arrived = shifted(memory_pairs, "segment", 1)
    crossed = lax.all_gather(attend(cross_queries, arrived), "mp", axis=1, tiled=True)
    decoded = (
        hidden_part.astype(jnp.float32) + project_out(crossed, cross_blocks)
    ).astype(jnp.bfloat16)
    chosen = jnp.where(lax.axis_index("segment") == 0, hidden_part, decoded)
    return chosen[None]


def solution(mesh):
    segments, blocks, parts = (mesh.shape["segment"], mesh.shape["blk"], mesh.shape["mp"])
    split = Mesh(
        mesh.devices.reshape(segments, blocks // X_SIZE, X_SIZE, parts),
        ("segment", "bz", "bx", "mp"),
    )
    rows = ("bz", "bx")
    return jax.shard_map(
        on_device,
        mesh=split,
        in_specs=(
            P("segment", rows, "mp"),
            P("segment", rows),
            P("segment", None, "mp"),
            P("segment", None),
            P("segment", None, None, "mp"),
            P("segment", "mp", None),
            P(),
            P(),
            P(None, None, "mp"),
            P("mp", None),
        ),
        out_specs=P("segment", rows, "mp"),
        check_vma=False,
    )
```

```python
import math

import jax
import jax.numpy as jnp
from jax import lax
from jax.experimental import pallas as pl
from jax.experimental.pallas import tpu as pltpu
from jax.sharding import Mesh
from jax.sharding import PartitionSpec as P

HEAD_DIM = 128
X_SIZE = 4
TILE = 256
STATS = 128
STAT_ROWS = 8


def shifted(value, axis, steps):
    count = lax.axis_size(axis)
    initial, last = (max(0, -steps), min(count, count - steps))
    return lax.ppermute(value, axis, [(source, source + steps) for source in range(initial, last)])


def rms_norm(values, gain):
    widened = values.astype(jnp.float32)
    meansq = jnp.mean(widened * widened, axis=-1, keepdims=True)
    return (widened * lax.rsqrt(meansq + 1e-05) * gain).astype(jnp.bfloat16)


def project(normed, weight):
    return jnp.dot(normed, weight, preferred_element_type=jnp.float32).astype(jnp.bfloat16)


def partial_kernel(q_ref, k_ref, v_ref, o_ref, s_ref):
    heads = q_ref.shape[1] // HEAD_DIM
    rows = q_ref.shape[0]
    lane = lax.broadcasted_iota(jnp.int32, (rows, STATS), 1)
    stats = jnp.zeros((rows, STATS), jnp.float32)
    for h in range(heads):
        cols = slice(h * HEAD_DIM, (h + 1) * HEAD_DIM)
        scores = lax.dot_general(
            q_ref[:, cols], k_ref[:, cols], (((1,), (1,)), ((), ())),
            preferred_element_type=jnp.float32,
        ) * (1.0 / math.sqrt(HEAD_DIM))
        largest = jnp.max(scores, axis=1, keepdims=True)
        weights = jnp.exp(scores - largest)
        summed = jnp.sum(weights, axis=1, keepdims=True)
        o_ref[:, cols] = jnp.dot(
            weights.astype(jnp.bfloat16), v_ref[:, cols], preferred_element_type=jnp.float32
        ).astype(o_ref.dtype)
        stats = jnp.where(lane == h, largest, stats)
        stats = jnp.where(lane == heads + h, summed, stats)
    s_ref[...] = jnp.transpose(stats)[: s_ref.shape[0]]


def partial_attend(queries, pairs):
    rows, width = queries.shape
    keys = pairs.shape[1]
    return pl.pallas_call(
        partial_kernel,
        grid=(rows // TILE,),
        in_specs=[
            pl.BlockSpec((TILE, width), lambda i: (i, 0)),
            pl.BlockSpec((None, keys, width), lambda i: (0, 0, 0)),
            pl.BlockSpec((None, keys, width), lambda i: (1, 0, 0)),
        ],
        out_specs=[
            pl.BlockSpec((TILE, width), lambda i: (i, 0)),
            pl.BlockSpec((STAT_ROWS, TILE), lambda i: (0, i)),
        ],
        out_shape=[
            jax.ShapeDtypeStruct((rows, width), jnp.bfloat16),
            jax.ShapeDtypeStruct((STAT_ROWS, rows), jnp.float32),
        ],
        compiler_params=pltpu.CompilerParams(vmem_limit_bytes=48 * 1024 * 1024),
    )(queries, pairs, pairs)


def attend(queries, pairs, riders=None):
    rows, width = queries.shape
    heads = width // HEAD_DIM
    query_block = lax.all_gather(queries, "bx", axis=0, tiled=True)
    key_block = lax.all_gather(pairs, "bz", axis=1, tiled=True)
    partial, stats = partial_attend(query_block, key_block)
    outs = lax.all_to_all(partial, "bx", 0, 0, tiled=True)
    stats = lax.all_to_all(stats, "bx", 1, 1, tiled=True)
    outs = outs.reshape(-1, rows, heads, HEAD_DIM).astype(jnp.float32)
    stats = stats.reshape(STAT_ROWS, -1, rows)
    maxes = jnp.transpose(stats[:heads], (1, 2, 0))
    sums = jnp.transpose(stats[heads:2 * heads], (1, 2, 0))
    top = jnp.max(maxes, axis=0)
    scale = jnp.exp(maxes - top[None])
    total = jnp.sum(sums * scale, axis=0)
    merged = jnp.sum(outs * scale[..., None], axis=0) / total[..., None]
    merged = merged.reshape(rows, width).astype(jnp.bfloat16)
    if riders is None:
        return merged
    return lax.optimization_barrier((merged, riders))


def spread(block_of):
    count = lax.axis_size("mp")
    me = lax.axis_index("mp")
    blocks = [(me, block_of(me))]
    for step in range(1, count):
        piece = block_of((me + step) % count)
        received = lax.ppermute(piece, "mp", [(j, (j + step) % count) for j in range(count)])
        blocks.append(((me - step + count) % count, received))
    return blocks


def project_out(attended_full, blocks):
    width = blocks[0][1].shape[0]
    total = None
    for source, block in blocks:
        piece = lax.dynamic_slice_in_dim(attended_full, source * width, width, axis=1)
        term = jnp.dot(piece, block, preferred_element_type=jnp.float32)
        total = term if total is None else total + term
    return total


def on_device(
    section_input,
    row_code,
    code_table,
    self_gain,
    self_weights,
    self_out,
    cross_gain,
    memory_gain,
    cross_weights,
    cross_out,
):
    local_rows = section_input.shape[1]
    local_width = section_input.shape[2]
    codes_total = code_table.shape[1]
    me = lax.axis_index("mp")
    self_blocks = spread(lambda target: self_out[0])
    cross_blocks = spread(
        lambda target: lax.dynamic_slice_in_dim(cross_out, target * local_width, local_width, axis=1)
    )
    matches = (
        row_code[0][:, None] == lax.broadcasted_iota(jnp.int32, (local_rows, codes_total), 1)
    ).astype(jnp.bfloat16)
    looked = jnp.dot(matches, code_table[0], preferred_element_type=jnp.float32)
    embedded = (section_input[0].astype(jnp.float32) + looked).astype(jnp.bfloat16)
    embedded_full = lax.all_gather(embedded, "mp", axis=1, tiled=True)
    normed = rms_norm(embedded_full, self_gain[0])
    self_queries = project(normed, self_weights[0, 0])
    self_pairs = jnp.stack(
        [project(normed, self_weights[0, 1]), project(normed, self_weights[0, 2])]
    )
    self_local, (self_blocks, cross_blocks) = attend(
        self_queries, self_pairs, (self_blocks, cross_blocks)
    )
    self_attended = lax.all_gather(self_local, "mp", axis=1, tiled=True)
    hidden_full = (
        embedded_full.astype(jnp.float32) + project_out(self_attended, self_blocks)
    ).astype(jnp.bfloat16)
    hidden_part = lax.dynamic_slice_in_dim(hidden_full, me * local_width, local_width, axis=1)
    cross_queries = project(rms_norm(hidden_full, cross_gain), cross_weights[0])
    memory_normed = rms_norm(hidden_full, memory_gain)
    memory_pairs = jnp.stack(
        [project(memory_normed, cross_weights[1]), project(memory_normed, cross_weights[2])]
    )
    arrived = shifted(memory_pairs, "segment", 1)
    crossed = lax.all_gather(attend(cross_queries, arrived), "mp", axis=1, tiled=True)
    decoded = (
        hidden_part.astype(jnp.float32) + project_out(crossed, cross_blocks)
    ).astype(jnp.bfloat16)
    chosen = jnp.where(lax.axis_index("segment") == 0, hidden_part, decoded)
    return chosen[None]


def solution(mesh):
    segments, blocks, parts = (mesh.shape["segment"], mesh.shape["blk"], mesh.shape["mp"])
    split = Mesh(
        mesh.devices.reshape(segments, blocks // X_SIZE, X_SIZE, parts),
        ("segment", "bz", "bx", "mp"),
    )
    rows = ("bz", "bx")
    return jax.shard_map(
        on_device,
        mesh=split,
        in_specs=(
            P("segment", rows, "mp"),
            P("segment", rows),
            P("segment", None, "mp"),
            P("segment", None),
            P("segment", None, None, "mp"),
            P("segment", "mp", None),
            P(),
            P(),
            P(None, None, "mp"),
            P("mp", None),
        ),
        out_specs=P("segment", rows, "mp"),
        check_vma=False,
    )
```

```python
import math

import jax
import jax.numpy as jnp
from jax import lax
from jax.experimental import pallas as pl
from jax.experimental.pallas import tpu as pltpu
from jax.sharding import Mesh
from jax.sharding import PartitionSpec as P

HEAD_DIM = 128
MP = ("my", "mc")
X_SIZE = 4
CORES = 2
TILE = 256
STATS = 128
STAT_ROWS = 8


def shifted(value, axis, steps):
    count = lax.axis_size(axis)
    initial, last = (max(0, -steps), min(count, count - steps))
    return lax.ppermute(value, axis, [(source, source + steps) for source in range(initial, last)])


def rms_norm(values, gain):
    widened = values.astype(jnp.float32)
    meansq = jnp.mean(widened * widened, axis=-1, keepdims=True)
    return (widened * lax.rsqrt(meansq + 1e-05) * gain).astype(jnp.bfloat16)


def project(normed, weight):
    return jnp.dot(normed, weight, preferred_element_type=jnp.float32).astype(jnp.bfloat16)


def partial_kernel(q_ref, k_ref, v_ref, o_ref, s_ref):
    heads = q_ref.shape[1] // HEAD_DIM
    rows = q_ref.shape[0]
    lane = lax.broadcasted_iota(jnp.int32, (rows, STATS), 1)
    stats = jnp.zeros((rows, STATS), jnp.float32)
    for h in range(heads):
        cols = slice(h * HEAD_DIM, (h + 1) * HEAD_DIM)
        scores = lax.dot_general(
            q_ref[:, cols], k_ref[:, cols], (((1,), (1,)), ((), ())),
            preferred_element_type=jnp.float32,
        ) * (1.0 / math.sqrt(HEAD_DIM))
        largest = jnp.max(scores, axis=1, keepdims=True)
        weights = jnp.exp(scores - largest)
        summed = jnp.sum(weights, axis=1, keepdims=True)
        o_ref[:, cols] = jnp.dot(
            weights.astype(jnp.bfloat16), v_ref[:, cols], preferred_element_type=jnp.float32
        ).astype(o_ref.dtype)
        stats = jnp.where(lane == h, largest, stats)
        stats = jnp.where(lane == heads + h, summed, stats)
    s_ref[...] = jnp.transpose(stats)[: s_ref.shape[0]]


def partial_attend(queries, pairs):
    rows, width = queries.shape
    keys = pairs.shape[1]
    return pl.pallas_call(
        partial_kernel,
        grid=(rows // TILE,),
        in_specs=[
            pl.BlockSpec((TILE, width), lambda i: (i, 0)),
            pl.BlockSpec((None, keys, width), lambda i: (0, 0, 0)),
            pl.BlockSpec((None, keys, width), lambda i: (1, 0, 0)),
        ],
        out_specs=[
            pl.BlockSpec((TILE, width), lambda i: (i, 0)),
            pl.BlockSpec((STAT_ROWS, TILE), lambda i: (0, i)),
        ],
        out_shape=[
            jax.ShapeDtypeStruct((rows, width), jnp.bfloat16),
            jax.ShapeDtypeStruct((STAT_ROWS, rows), jnp.float32),
        ],
        compiler_params=pltpu.CompilerParams(vmem_limit_bytes=48 * 1024 * 1024),
    )(queries, pairs, pairs)


def attend(queries, pairs, riders=None):
    rows, width = queries.shape
    heads = width // HEAD_DIM
    query_block = lax.all_gather(queries, "bx", axis=0, tiled=True)
    key_block = lax.all_gather(pairs, "bz", axis=1, tiled=True)
    partial, stats = partial_attend(query_block, key_block)
    outs = lax.all_to_all(partial, "bx", 0, 0, tiled=True)
    stats = lax.all_to_all(stats, "bx", 1, 1, tiled=True)
    outs = outs.reshape(-1, rows, heads, HEAD_DIM).astype(jnp.float32)
    stats = stats.reshape(STAT_ROWS, -1, rows)
    maxes = jnp.transpose(stats[:heads], (1, 2, 0))
    sums = jnp.transpose(stats[heads:2 * heads], (1, 2, 0))
    top = jnp.max(maxes, axis=0)
    scale = jnp.exp(maxes - top[None])
    total = jnp.sum(sums * scale, axis=0)
    merged = jnp.sum(outs * scale[..., None], axis=0) / total[..., None]
    merged = merged.reshape(rows, width).astype(jnp.bfloat16)
    if riders is None:
        return merged
    return lax.optimization_barrier((merged, riders))


def mp_index():
    return lax.axis_index("my") * lax.axis_size("mc") + lax.axis_index("mc")


def mp_gather(value):
    across = lax.all_gather(value, "my", axis=1, tiled=True)
    both = lax.all_gather(across, "mc", axis=1, tiled=True)
    rows, width = value.shape
    grouped = both.reshape(rows, lax.axis_size("mc"), lax.axis_size("my"), width)
    return grouped.transpose(0, 2, 1, 3).reshape(rows, -1)


def spread(block_of):
    count = lax.axis_size("my") * lax.axis_size("mc")
    me = mp_index()
    sources, blocks = [me], [block_of(me)]
    for step in range(1, count):
        piece = block_of((me + step) % count)
        received = lax.ppermute(piece, MP, [(j, (j + step) % count) for j in range(count)])
        sources.append((me - step + count) % count)
        blocks.append(received)
    return jnp.stack(sources), jnp.concatenate(blocks, axis=0)


def project_out(attended_full, spread_weight):
    sources, weight = spread_weight
    width = weight.shape[0] // sources.shape[0]
    pieces = [
        lax.dynamic_slice_in_dim(attended_full, sources[i] * width, width, axis=1)
        for i in range(sources.shape[0])
    ]
    return jnp.dot(jnp.concatenate(pieces, axis=1), weight, preferred_element_type=jnp.float32)


def on_device(
    section_input,
    row_code,
    code_table,
    self_gain,
    self_weights,
    self_out,
    cross_gain,
    memory_gain,
    cross_weights,
    cross_out,
):
    local_rows = section_input.shape[1]
    local_width = section_input.shape[2]
    codes_total = code_table.shape[1]
    me = mp_index()
    self_blocks = spread(lambda target: self_out[0])
    cross_blocks = spread(
        lambda target: lax.dynamic_slice_in_dim(cross_out, target * local_width, local_width, axis=1)
    )
    matches = (
        row_code[0][:, None] == lax.broadcasted_iota(jnp.int32, (local_rows, codes_total), 1)
    ).astype(jnp.bfloat16)
    looked = jnp.dot(matches, code_table[0], preferred_element_type=jnp.float32)
    embedded = (section_input[0].astype(jnp.float32) + looked).astype(jnp.bfloat16)
    embedded_full = mp_gather(embedded)
    normed = rms_norm(embedded_full, self_gain[0])
    self_queries = project(normed, self_weights[0, 0])
    self_pairs = jnp.stack(
        [project(normed, self_weights[0, 1]), project(normed, self_weights[0, 2])]
    )
    self_local, (self_blocks, cross_blocks) = attend(
        self_queries, self_pairs, (self_blocks, cross_blocks)
    )
    self_attended = mp_gather(self_local)
    hidden_full = (
        embedded_full.astype(jnp.float32) + project_out(self_attended, self_blocks)
    ).astype(jnp.bfloat16)
    hidden_part = lax.dynamic_slice_in_dim(hidden_full, me * local_width, local_width, axis=1)
    cross_queries = project(rms_norm(hidden_full, cross_gain), cross_weights[0])
    memory_normed = rms_norm(hidden_full, memory_gain)
    memory_pairs = jnp.stack(
        [project(memory_normed, cross_weights[1]), project(memory_normed, cross_weights[2])]
    )
    arrived = shifted(memory_pairs, "segment", 1)
    crossed = mp_gather(attend(cross_queries, arrived))
    decoded = (
        hidden_part.astype(jnp.float32) + project_out(crossed, cross_blocks)
    ).astype(jnp.bfloat16)
    chosen = jnp.where(lax.axis_index("segment") == 0, hidden_part, decoded)
    return chosen[None]


def solution(mesh):
    segments, blocks, parts = (mesh.shape["segment"], mesh.shape["blk"], mesh.shape["mp"])
    split = Mesh(
        mesh.devices.reshape(segments, blocks // X_SIZE, X_SIZE, parts // CORES, CORES),
        ("segment", "bz", "bx", "my", "mc"),
    )
    rows = ("bz", "bx")
    return jax.shard_map(
        on_device,
        mesh=split,
        in_specs=(
            P("segment", rows, MP),
            P("segment", rows),
            P("segment", None, MP),
            P("segment", None),
            P("segment", None, None, MP),
            P("segment", MP, None),
            P(),
            P(),
            P(None, None, MP),
            P(MP, None),
        ),
        out_specs=P("segment", rows, MP),
        check_vma=False,
    )
```

```python
import math

import jax
import jax.numpy as jnp
from jax import lax
from jax.experimental import pallas as pl
from jax.experimental.pallas import tpu as pltpu
from jax.sharding import Mesh
from jax.sharding import PartitionSpec as P

HEAD_DIM = 128
X_SIZE = 4
TILE = 256
STATS = 128
PARTS = 3


def shifted(value, axis, steps):
    count = lax.axis_size(axis)
    initial, last = (max(0, -steps), min(count, count - steps))
    return lax.ppermute(value, axis, [(source, source + steps) for source in range(initial, last)])


def rms_norm(values, gain):
    widened = values.astype(jnp.float32)
    meansq = jnp.mean(widened * widened, axis=-1, keepdims=True)
    return (widened * lax.rsqrt(meansq + 1e-05) * gain).astype(jnp.bfloat16)


def project(normed, weight):
    return jnp.dot(normed, weight, preferred_element_type=jnp.float32).astype(jnp.bfloat16)


def split_parts(value, count):
    parts = []
    rest = value
    for unused in range(count):
        part = rest.astype(jnp.bfloat16).astype(jnp.float32)
        parts.append(part)
        rest = rest - part
    return parts


def partial_kernel(q_ref, k_ref, v_ref, o_ref):
    heads = q_ref.shape[1] // HEAD_DIM
    rows = q_ref.shape[0]
    lane = lax.broadcasted_iota(jnp.int32, (rows, STATS), 1)
    stats = jnp.zeros((rows, STATS), jnp.float32)
    for h in range(heads):
        cols = slice(h * HEAD_DIM, (h + 1) * HEAD_DIM)
        scores = lax.dot_general(
            q_ref[:, cols], k_ref[:, cols], (((1,), (1,)), ((), ())),
            preferred_element_type=jnp.float32,
        ) * (1.0 / math.sqrt(HEAD_DIM))
        largest = jnp.max(scores, axis=1, keepdims=True)
        weights = jnp.exp(scores - largest)
        summed = jnp.sum(weights, axis=1, keepdims=True)
        o_ref[:, cols] = jnp.dot(
            weights.astype(jnp.bfloat16), v_ref[:, cols], preferred_element_type=jnp.float32
        ).astype(o_ref.dtype)
        for kind, value in enumerate((largest, summed)):
            for piece, part in enumerate(split_parts(value, PARTS)):
                slot = (kind * heads + h) * PARTS + piece
                stats = jnp.where(lane == slot, part, stats)
    o_ref[:, heads * HEAD_DIM:] = stats.astype(o_ref.dtype)


def partial_attend(queries, pairs):
    rows, width = queries.shape
    keys = pairs.shape[1]
    return pl.pallas_call(
        partial_kernel,
        grid=(rows // TILE,),
        in_specs=[
            pl.BlockSpec((TILE, width), lambda i: (i, 0)),
            pl.BlockSpec((None, keys, width), lambda i: (0, 0, 0)),
            pl.BlockSpec((None, keys, width), lambda i: (1, 0, 0)),
        ],
        out_specs=pl.BlockSpec((TILE, width + STATS), lambda i: (i, 0)),
        out_shape=jax.ShapeDtypeStruct((rows, width + STATS), jnp.bfloat16),
        compiler_params=pltpu.CompilerParams(vmem_limit_bytes=48 * 1024 * 1024),
    )(queries, pairs, pairs)


def attend(queries, pairs, riders=None):
    rows, width = queries.shape
    heads = width // HEAD_DIM
    query_block = lax.all_gather(queries, "bx", axis=0, tiled=True)
    key_block = lax.all_gather(pairs, "bz", axis=1, tiled=True)
    partial = partial_attend(query_block, key_block)
    parts = lax.all_to_all(partial, "bx", 0, 0, tiled=True)
    parts = parts.reshape(-1, rows, width + STATS).astype(jnp.float32)
    outs = parts[:, :, :width].reshape(-1, rows, heads, HEAD_DIM)
    stats = parts[:, :, width:width + 2 * heads * PARTS].reshape(-1, rows, 2, heads, PARTS)
    stats = jnp.sum(stats, axis=-1)
    maxes = stats[:, :, 0]
    sums = stats[:, :, 1]
    top = jnp.max(maxes, axis=0)
    scale = jnp.exp(maxes - top[None])
    total = jnp.sum(sums * scale, axis=0)
    merged = jnp.sum(outs * scale[..., None], axis=0) / total[..., None]
    merged = merged.reshape(rows, width).astype(jnp.bfloat16)
    if riders is None:
        return merged
    return lax.optimization_barrier((merged, riders))


def spread(block_of):
    count = lax.axis_size("mp")
    me = lax.axis_index("mp")
    blocks = [(me, block_of(me))]
    for step in range(1, count):
        piece = block_of((me + step) % count)
        received = lax.ppermute(piece, "mp", [(j, (j + step) % count) for j in range(count)])
        blocks.append(((me - step + count) % count, received))
    return blocks


def project_out(attended_full, blocks):
    width = blocks[0][1].shape[0]
    total = None
    for source, block in blocks:
        piece = lax.dynamic_slice_in_dim(attended_full, source * width, width, axis=1)
        term = jnp.dot(piece, block, preferred_element_type=jnp.float32)
        total = term if total is None else total + term
    return total


def on_device(
    section_input,
    row_code,
    code_table,
    self_gain,
    self_weights,
    self_out,
    cross_gain,
    memory_gain,
    cross_weights,
    cross_out,
):
    local_rows = section_input.shape[1]
    local_width = section_input.shape[2]
    codes_total = code_table.shape[1]
    me = lax.axis_index("mp")
    self_blocks = spread(lambda target: self_out[0])
    cross_blocks = spread(
        lambda target: lax.dynamic_slice_in_dim(cross_out, target * local_width, local_width, axis=1)
    )
    matches = (
        row_code[0][:, None] == lax.broadcasted_iota(jnp.int32, (local_rows, codes_total), 1)
    ).astype(jnp.bfloat16)
    looked = jnp.dot(matches, code_table[0], preferred_element_type=jnp.float32)
    embedded = (section_input[0].astype(jnp.float32) + looked).astype(jnp.bfloat16)
    embedded_full = lax.all_gather(embedded, "mp", axis=1, tiled=True)
    normed = rms_norm(embedded_full, self_gain[0])
    self_queries = project(normed, self_weights[0, 0])
    self_pairs = jnp.stack(
        [project(normed, self_weights[0, 1]), project(normed, self_weights[0, 2])]
    )
    self_local, (self_blocks, cross_blocks) = attend(
        self_queries, self_pairs, (self_blocks, cross_blocks)
    )
    self_attended = lax.all_gather(self_local, "mp", axis=1, tiled=True)
    hidden_full = (
        embedded_full.astype(jnp.float32) + project_out(self_attended, self_blocks)
    ).astype(jnp.bfloat16)
    hidden_part = lax.dynamic_slice_in_dim(hidden_full, me * local_width, local_width, axis=1)
    cross_queries = project(rms_norm(hidden_full, cross_gain), cross_weights[0])
    memory_normed = rms_norm(hidden_full, memory_gain)
    memory_pairs = jnp.stack(
        [project(memory_normed, cross_weights[1]), project(memory_normed, cross_weights[2])]
    )
    arrived = shifted(memory_pairs, "segment", 1)
    crossed = lax.all_gather(attend(cross_queries, arrived), "mp", axis=1, tiled=True)
    decoded = (
        hidden_part.astype(jnp.float32) + project_out(crossed, cross_blocks)
    ).astype(jnp.bfloat16)
    chosen = jnp.where(lax.axis_index("segment") == 0, hidden_part, decoded)
    return chosen[None]


def solution(mesh):
    segments, blocks, parts = (mesh.shape["segment"], mesh.shape["blk"], mesh.shape["mp"])
    split = Mesh(
        mesh.devices.reshape(segments, blocks // X_SIZE, X_SIZE, parts),
        ("segment", "bz", "bx", "mp"),
    )
    rows = ("bz", "bx")
    return jax.shard_map(
        on_device,
        mesh=split,
        in_specs=(
            P("segment", rows, "mp"),
            P("segment", rows),
            P("segment", None, "mp"),
            P("segment", None),
            P("segment", None, None, "mp"),
            P("segment", "mp", None),
            P(),
            P(),
            P(None, None, "mp"),
            P("mp", None),
        ),
        out_specs=P("segment", rows, "mp"),
        check_vma=False,
    )
```

```python
import math

import jax
import jax.numpy as jnp
from jax import lax
from jax.experimental import pallas as pl
from jax.experimental.pallas import tpu as pltpu
from jax.sharding import Mesh
from jax.sharding import PartitionSpec as P

HEAD_DIM = 128
X_SIZE = 4
TILE = 256
STATS = 128
PARTS = 3


def shifted(value, axis, steps):
    count = lax.axis_size(axis)
    initial, last = (max(0, -steps), min(count, count - steps))
    return lax.ppermute(value, axis, [(source, source + steps) for source in range(initial, last)])


def rms_norm(values, gain):
    widened = values.astype(jnp.float32)
    meansq = jnp.mean(widened * widened, axis=-1, keepdims=True)
    return (widened * lax.rsqrt(meansq + 1e-05) * gain).astype(jnp.bfloat16)


def project(normed, weight):
    return jnp.dot(normed, weight, preferred_element_type=jnp.float32).astype(jnp.bfloat16)


def split_parts(value, count):
    parts = []
    rest = value
    for unused in range(count):
        part = rest.astype(jnp.bfloat16).astype(jnp.float32)
        parts.append(part)
        rest = rest - part
    return parts


def partial_kernel(q_ref, k_ref, v_ref, o_ref):
    heads = q_ref.shape[1] // HEAD_DIM
    rows = q_ref.shape[0]
    lane = lax.broadcasted_iota(jnp.int32, (rows, STATS), 1)
    stats = jnp.zeros((rows, STATS), jnp.float32)
    for h in range(heads):
        cols = slice(h * HEAD_DIM, (h + 1) * HEAD_DIM)
        scores = lax.dot_general(
            q_ref[:, cols], k_ref[:, cols], (((1,), (1,)), ((), ())),
            preferred_element_type=jnp.float32,
        ) * (1.0 / math.sqrt(HEAD_DIM))
        largest = jnp.max(scores, axis=1, keepdims=True)
        weights = jnp.exp(scores - largest)
        summed = jnp.sum(weights, axis=1, keepdims=True)
        o_ref[:, cols] = jnp.dot(
            weights.astype(jnp.bfloat16), v_ref[:, cols], preferred_element_type=jnp.float32
        ).astype(o_ref.dtype)
        for kind, value in enumerate((largest, summed)):
            for piece, part in enumerate(split_parts(value, PARTS)):
                slot = (kind * heads + h) * PARTS + piece
                stats = jnp.where(lane == slot, part, stats)
    o_ref[:, heads * HEAD_DIM:] = stats.astype(o_ref.dtype)


def partial_attend(queries, pairs):
    rows, width = queries.shape
    keys = pairs.shape[1]
    return pl.pallas_call(
        partial_kernel,
        grid=(rows // TILE,),
        in_specs=[
            pl.BlockSpec((TILE, width), lambda i: (i, 0)),
            pl.BlockSpec((None, keys, width), lambda i: (0, 0, 0)),
            pl.BlockSpec((None, keys, width), lambda i: (1, 0, 0)),
        ],
        out_specs=pl.BlockSpec((TILE, width + STATS), lambda i: (i, 0)),
        out_shape=jax.ShapeDtypeStruct((rows, width + STATS), jnp.bfloat16),
        compiler_params=pltpu.CompilerParams(vmem_limit_bytes=48 * 1024 * 1024),
    )(queries, pairs, pairs)


def attend(queries, pairs, riders=None):
    rows, width = queries.shape
    heads = width // HEAD_DIM
    query_block = lax.all_gather(queries, "bx", axis=0, tiled=True)
    key_block = lax.all_gather(pairs, "bz", axis=1, tiled=True)
    partial = partial_attend(query_block, key_block)
    if riders is not None:
        partial, riders = lax.optimization_barrier((partial, riders))
    parts = lax.all_to_all(partial, "bx", 0, 0, tiled=True)
    parts = parts.reshape(-1, rows, width + STATS).astype(jnp.float32)
    outs = parts[:, :, :width].reshape(-1, rows, heads, HEAD_DIM)
    stats = parts[:, :, width:width + 2 * heads * PARTS].reshape(-1, rows, 2, heads, PARTS)
    stats = jnp.sum(stats, axis=-1)
    maxes = stats[:, :, 0]
    sums = stats[:, :, 1]
    top = jnp.max(maxes, axis=0)
    scale = jnp.exp(maxes - top[None])
    total = jnp.sum(sums * scale, axis=0)
    merged = jnp.sum(outs * scale[..., None], axis=0) / total[..., None]
    merged = merged.reshape(rows, width).astype(jnp.bfloat16)
    return merged if riders is None else (merged, riders)


def spread(block_of):
    count = lax.axis_size("mp")
    me = lax.axis_index("mp")
    blocks = [(me, block_of(me))]
    for step in range(1, count):
        piece = block_of((me + step) % count)
        received = lax.ppermute(piece, "mp", [(j, (j + step) % count) for j in range(count)])
        blocks.append(((me - step + count) % count, received))
    return blocks


def project_out(attended_full, blocks):
    width = blocks[0][1].shape[0]
    pieces = [
        lax.dynamic_slice_in_dim(attended_full, source * width, width, axis=1)
        for source, unused in blocks
    ]
    weight = jnp.concatenate([block for unused, block in blocks], axis=0)
    return jnp.dot(jnp.concatenate(pieces, axis=1), weight, preferred_element_type=jnp.float32)


def on_device(
    section_input,
    row_code,
    code_table,
    self_gain,
    self_weights,
    self_out,
    cross_gain,
    memory_gain,
    cross_weights,
    cross_out,
):
    local_rows = section_input.shape[1]
    local_width = section_input.shape[2]
    codes_total = code_table.shape[1]
    me = lax.axis_index("mp")
    self_blocks = spread(lambda target: self_out[0])
    cross_blocks = spread(
        lambda target: lax.dynamic_slice_in_dim(cross_out, target * local_width, local_width, axis=1)
    )
    matches = (
        row_code[0][:, None] == lax.broadcasted_iota(jnp.int32, (local_rows, codes_total), 1)
    ).astype(jnp.bfloat16)
    looked = jnp.dot(matches, code_table[0], preferred_element_type=jnp.float32)
    embedded = (section_input[0].astype(jnp.float32) + looked).astype(jnp.bfloat16)
    embedded_full = lax.all_gather(embedded, "mp", axis=1, tiled=True)
    normed = rms_norm(embedded_full, self_gain[0])
    self_queries = project(normed, self_weights[0, 0])
    self_pairs = jnp.stack(
        [project(normed, self_weights[0, 1]), project(normed, self_weights[0, 2])]
    )
    self_local, (self_blocks, cross_blocks) = attend(
        self_queries, self_pairs, (self_blocks, cross_blocks)
    )
    self_attended = lax.all_gather(self_local, "mp", axis=1, tiled=True)
    hidden_full = (
        embedded_full.astype(jnp.float32) + project_out(self_attended, self_blocks)
    ).astype(jnp.bfloat16)
    hidden_part = lax.dynamic_slice_in_dim(hidden_full, me * local_width, local_width, axis=1)
    cross_queries = project(rms_norm(hidden_full, cross_gain), cross_weights[0])
    memory_normed = rms_norm(hidden_full, memory_gain)
    memory_pairs = jnp.stack(
        [project(memory_normed, cross_weights[1]), project(memory_normed, cross_weights[2])]
    )
    arrived = shifted(memory_pairs, "segment", 1)
    crossed = lax.all_gather(attend(cross_queries, arrived), "mp", axis=1, tiled=True)
    decoded = (
        hidden_part.astype(jnp.float32) + project_out(crossed, cross_blocks)
    ).astype(jnp.bfloat16)
    chosen = jnp.where(lax.axis_index("segment") == 0, hidden_part, decoded)
    return chosen[None]


def solution(mesh):
    segments, blocks, parts = (mesh.shape["segment"], mesh.shape["blk"], mesh.shape["mp"])
    split = Mesh(
        mesh.devices.reshape(segments, blocks // X_SIZE, X_SIZE, parts),
        ("segment", "bz", "bx", "mp"),
    )
    rows = ("bz", "bx")
    return jax.shard_map(
        on_device,
        mesh=split,
        in_specs=(
            P("segment", rows, "mp"),
            P("segment", rows),
            P("segment", None, "mp"),
            P("segment", None),
            P("segment", None, None, "mp"),
            P("segment", "mp", None),
            P(),
            P(),
            P(None, None, "mp"),
            P("mp", None),
        ),
        out_specs=P("segment", rows, "mp"),
        check_vma=False,
    )
```

```python
import math

import jax
import jax.numpy as jnp
from jax import lax
from jax.experimental import pallas as pl
from jax.experimental.pallas import tpu as pltpu
from jax.sharding import Mesh
from jax.sharding import PartitionSpec as P

HEAD_DIM = 128
MP = ("my", "mc")
X_SIZE = 4
CORES = 2
TILE = 256
STATS = 128
PARTS = 3


def shifted(value, axis, steps):
    count = lax.axis_size(axis)
    initial, last = (max(0, -steps), min(count, count - steps))
    return lax.ppermute(value, axis, [(source, source + steps) for source in range(initial, last)])


def rms_norm(values, gain):
    widened = values.astype(jnp.float32)
    meansq = jnp.mean(widened * widened, axis=-1, keepdims=True)
    return (widened * lax.rsqrt(meansq + 1e-05) * gain).astype(jnp.bfloat16)


def project(normed, weight):
    return jnp.dot(normed, weight, preferred_element_type=jnp.float32).astype(jnp.bfloat16)


def split_parts(value, count):
    parts = []
    rest = value
    for unused in range(count):
        part = rest.astype(jnp.bfloat16).astype(jnp.float32)
        parts.append(part)
        rest = rest - part
    return parts


def partial_kernel(q_ref, k_ref, v_ref, o_ref):
    heads = q_ref.shape[1] // HEAD_DIM
    rows = q_ref.shape[0]
    lane = lax.broadcasted_iota(jnp.int32, (rows, STATS), 1)
    stats = jnp.zeros((rows, STATS), jnp.float32)
    for h in range(heads):
        cols = slice(h * HEAD_DIM, (h + 1) * HEAD_DIM)
        scores = lax.dot_general(
            q_ref[:, cols], k_ref[:, cols], (((1,), (1,)), ((), ())),
            preferred_element_type=jnp.float32,
        ) * (1.0 / math.sqrt(HEAD_DIM))
        largest = jnp.max(scores, axis=1, keepdims=True)
        weights = jnp.exp(scores - largest)
        summed = jnp.sum(weights, axis=1, keepdims=True)
        o_ref[:, cols] = jnp.dot(
            weights.astype(jnp.bfloat16), v_ref[:, cols], preferred_element_type=jnp.float32
        ).astype(o_ref.dtype)
        for kind, value in enumerate((largest, summed)):
            for piece, part in enumerate(split_parts(value, PARTS)):
                slot = (kind * heads + h) * PARTS + piece
                stats = jnp.where(lane == slot, part, stats)
    o_ref[:, heads * HEAD_DIM:] = stats.astype(o_ref.dtype)


def partial_attend(queries, pairs):
    rows, width = queries.shape
    keys = pairs.shape[1]
    return pl.pallas_call(
        partial_kernel,
        grid=(rows // TILE,),
        in_specs=[
            pl.BlockSpec((TILE, width), lambda i: (i, 0)),
            pl.BlockSpec((None, keys, width), lambda i: (0, 0, 0)),
            pl.BlockSpec((None, keys, width), lambda i: (1, 0, 0)),
        ],
        out_specs=pl.BlockSpec((TILE, width + STATS), lambda i: (i, 0)),
        out_shape=jax.ShapeDtypeStruct((rows, width + STATS), jnp.bfloat16),
        compiler_params=pltpu.CompilerParams(vmem_limit_bytes=48 * 1024 * 1024),
    )(queries, pairs, pairs)


def attend(queries, pairs, riders=None):
    rows, width = queries.shape
    heads = width // HEAD_DIM
    query_block = lax.all_gather(queries, "bx", axis=0, tiled=True)
    key_block = lax.all_gather(pairs, "bz", axis=1, tiled=True)
    partial = partial_attend(query_block, key_block)
    if riders is not None:
        partial, riders = lax.optimization_barrier((partial, riders))
    parts = lax.all_to_all(partial, "bx", 0, 0, tiled=True)
    parts = parts.reshape(-1, rows, width + STATS).astype(jnp.float32)
    outs = parts[:, :, :width].reshape(-1, rows, heads, HEAD_DIM)
    stats = parts[:, :, width:width + 2 * heads * PARTS].reshape(-1, rows, 2, heads, PARTS)
    stats = jnp.sum(stats, axis=-1)
    maxes = stats[:, :, 0]
    sums = stats[:, :, 1]
    top = jnp.max(maxes, axis=0)
    scale = jnp.exp(maxes - top[None])
    total = jnp.sum(sums * scale, axis=0)
    merged = jnp.sum(outs * scale[..., None], axis=0) / total[..., None]
    merged = merged.reshape(rows, width).astype(jnp.bfloat16)
    return merged if riders is None else (merged, riders)


def spread(block_of):
    count = lax.axis_size(MP)
    me = lax.axis_index(MP)
    blocks = [(me, block_of(me))]
    for step in range(1, count):
        piece = block_of((me + step) % count)
        received = lax.ppermute(piece, MP, [(j, (j + step) % count) for j in range(count)])
        blocks.append(((me - step + count) % count, received))
    return blocks


def spread_rows(block):
    other = lax.ppermute(block, "my", [(0, 1), (1, 0)])
    near = lax.ppermute(block, "mc", [(0, 1), (1, 0)])
    return other, near


def rows_in_order(block, other, near):
    my, mc = lax.axis_index("my"), lax.axis_index("mc")
    cores = lax.axis_size("mc")
    far = lax.ppermute(other, "mc", [(0, 1), (1, 0)])
    return [
        (my * cores + mc, block),
        ((1 - my) * cores + mc, other),
        (my * cores + 1 - mc, near),
        ((1 - my) * cores + 1 - mc, far),
    ]


def project_out(attended_full, blocks):
    width = blocks[0][1].shape[0]
    pieces = [
        lax.dynamic_slice_in_dim(attended_full, source * width, width, axis=1)
        for source, unused in blocks
    ]
    weight = jnp.concatenate([block for unused, block in blocks], axis=0)
    return jnp.dot(jnp.concatenate(pieces, axis=1), weight, preferred_element_type=jnp.float32)


def on_device(
    section_input,
    row_code,
    code_table,
    self_gain,
    self_weights,
    self_out,
    cross_gain,
    memory_gain,
    cross_weights,
    cross_out,
):
    local_rows = section_input.shape[1]
    local_width = section_input.shape[2]
    codes_total = code_table.shape[1]
    me = lax.axis_index(MP)
    self_other, self_near = spread_rows(self_out[0])
    cross_blocks = spread(
        lambda target: lax.dynamic_slice_in_dim(cross_out, target * local_width, local_width, axis=1)
    )
    matches = (
        row_code[0][:, None] == lax.broadcasted_iota(jnp.int32, (local_rows, codes_total), 1)
    ).astype(jnp.bfloat16)
    looked = jnp.dot(matches, code_table[0], preferred_element_type=jnp.float32)
    embedded = (section_input[0].astype(jnp.float32) + looked).astype(jnp.bfloat16)
    embedded_full = lax.all_gather(embedded, MP, axis=1, tiled=True)
    normed = rms_norm(embedded_full, self_gain[0])
    self_queries = project(normed, self_weights[0, 0])
    self_pairs = jnp.stack(
        [project(normed, self_weights[0, 1]), project(normed, self_weights[0, 2])]
    )
    self_local, (self_other, self_near, cross_blocks) = attend(
        self_queries, self_pairs, (self_other, self_near, cross_blocks)
    )
    self_blocks = rows_in_order(self_out[0], self_other, self_near)
    self_attended = lax.all_gather(self_local, MP, axis=1, tiled=True)
    hidden_full = (
        embedded_full.astype(jnp.float32) + project_out(self_attended, self_blocks)
    ).astype(jnp.bfloat16)
    hidden_part = lax.dynamic_slice_in_dim(hidden_full, me * local_width, local_width, axis=1)
    cross_queries = project(rms_norm(hidden_full, cross_gain), cross_weights[0])
    memory_normed = rms_norm(hidden_full, memory_gain)
    memory_pairs = jnp.stack(
        [project(memory_normed, cross_weights[1]), project(memory_normed, cross_weights[2])]
    )
    arrived = shifted(memory_pairs, "segment", 1)
    crossed = lax.all_gather(attend(cross_queries, arrived), MP, axis=1, tiled=True)
    decoded = (
        hidden_part.astype(jnp.float32) + project_out(crossed, cross_blocks)
    ).astype(jnp.bfloat16)
    chosen = jnp.where(lax.axis_index("segment") == 0, hidden_part, decoded)
    return chosen[None]


def solution(mesh):
    segments, blocks, parts = (mesh.shape["segment"], mesh.shape["blk"], mesh.shape["mp"])
    split = Mesh(
        mesh.devices.reshape(segments, blocks // X_SIZE, X_SIZE, parts // CORES, CORES),
        ("segment", "bz", "bx", "my", "mc"),
    )
    rows = ("bz", "bx")
    return jax.shard_map(
        on_device,
        mesh=split,
        in_specs=(
            P("segment", rows, MP),
            P("segment", rows),
            P("segment", None, MP),
            P("segment", None),
            P("segment", None, None, MP),
            P("segment", MP, None),
            P(),
            P(),
            P(None, None, MP),
            P(MP, None),
        ),
        out_specs=P("segment", rows, MP),
        check_vma=False,
    )
```

```python
import math

import jax
import jax.numpy as jnp
from jax import lax
from jax.experimental import pallas as pl
from jax.experimental.pallas import tpu as pltpu
from jax.sharding import Mesh
from jax.sharding import PartitionSpec as P

HEAD_DIM = 128
MP = ("my", "mc")
X_SIZE = 4
CORES = 2
TILE = 256
STATS = 128
PARTS = 3


def shifted(value, axis, steps):
    count = lax.axis_size(axis)
    initial, last = (max(0, -steps), min(count, count - steps))
    return lax.ppermute(value, axis, [(source, source + steps) for source in range(initial, last)])


def rms_norm(values, gain):
    widened = values.astype(jnp.float32)
    meansq = jnp.mean(widened * widened, axis=-1, keepdims=True)
    return (widened * lax.rsqrt(meansq + 1e-05) * gain).astype(jnp.bfloat16)


def project(normed, weight):
    return jnp.dot(normed, weight, preferred_element_type=jnp.float32).astype(jnp.bfloat16)


def split_parts(value, count):
    parts = []
    rest = value
    for unused in range(count):
        part = rest.astype(jnp.bfloat16).astype(jnp.float32)
        parts.append(part)
        rest = rest - part
    return parts


def partial_kernel(q_ref, k_ref, v_ref, o_ref):
    heads = q_ref.shape[1] // HEAD_DIM
    rows = q_ref.shape[0]
    lane = lax.broadcasted_iota(jnp.int32, (rows, STATS), 1)
    stats = jnp.zeros((rows, STATS), jnp.float32)
    for h in range(heads):
        cols = slice(h * HEAD_DIM, (h + 1) * HEAD_DIM)
        scores = lax.dot_general(
            q_ref[:, cols], k_ref[:, cols], (((1,), (1,)), ((), ())),
            preferred_element_type=jnp.float32,
        ) * (1.0 / math.sqrt(HEAD_DIM))
        largest = jnp.max(scores, axis=1, keepdims=True)
        weights = jnp.exp(scores - largest)
        summed = jnp.sum(weights, axis=1, keepdims=True)
        o_ref[:, cols] = jnp.dot(
            weights.astype(jnp.bfloat16), v_ref[:, cols], preferred_element_type=jnp.float32
        ).astype(o_ref.dtype)
        for kind, value in enumerate((largest, summed)):
            for piece, part in enumerate(split_parts(value, PARTS)):
                slot = (kind * heads + h) * PARTS + piece
                stats = jnp.where(lane == slot, part, stats)
    o_ref[:, heads * HEAD_DIM:] = stats.astype(o_ref.dtype)


def partial_attend(queries, pairs):
    rows, width = queries.shape
    keys = pairs.shape[1]
    return pl.pallas_call(
        partial_kernel,
        grid=(rows // TILE,),
        in_specs=[
            pl.BlockSpec((TILE, width), lambda i: (i, 0)),
            pl.BlockSpec((None, keys, width), lambda i: (0, 0, 0)),
            pl.BlockSpec((None, keys, width), lambda i: (1, 0, 0)),
        ],
        out_specs=pl.BlockSpec((TILE, width + STATS), lambda i: (i, 0)),
        out_shape=jax.ShapeDtypeStruct((rows, width + STATS), jnp.bfloat16),
        compiler_params=pltpu.CompilerParams(vmem_limit_bytes=48 * 1024 * 1024),
    )(queries, pairs, pairs)


def attend(queries, pairs, riders=None):
    rows, width = queries.shape
    heads = width // HEAD_DIM
    query_block = lax.all_gather(queries, "bx", axis=0, tiled=True)
    key_block = lax.all_gather(pairs, "bz", axis=1, tiled=True)
    partial = partial_attend(query_block, key_block)
    if riders is not None:
        partial, riders = lax.optimization_barrier((partial, riders))
    count = lax.axis_size("bx")
    me = lax.axis_index("bx")
    chunks = [lax.dynamic_slice_in_dim(partial, me * rows, rows, axis=0)]
    for step in range(1, count):
        piece = lax.dynamic_slice_in_dim(partial, ((me + step) % count) * rows, rows, axis=0)
        chunks.append(
            lax.ppermute(piece, "bx", [(j, (j + step) % count) for j in range(count)])
        )
    parts = jnp.stack(chunks).astype(jnp.float32)
    outs = parts[:, :, :width].reshape(-1, rows, heads, HEAD_DIM)
    stats = parts[:, :, width:width + 2 * heads * PARTS].reshape(-1, rows, 2, heads, PARTS)
    stats = jnp.sum(stats, axis=-1)
    maxes = stats[:, :, 0]
    sums = stats[:, :, 1]
    top = jnp.max(maxes, axis=0)
    scale = jnp.exp(maxes - top[None])
    total = jnp.sum(sums * scale, axis=0)
    merged = jnp.sum(outs * scale[..., None], axis=0) / total[..., None]
    merged = merged.reshape(rows, width).astype(jnp.bfloat16)
    return merged if riders is None else (merged, riders)


def spread(block_of):
    count = lax.axis_size(MP)
    me = lax.axis_index(MP)
    blocks = [(me, block_of(me))]
    for step in range(1, count):
        piece = block_of((me + step) % count)
        received = lax.ppermute(piece, MP, [(j, (j + step) % count) for j in range(count)])
        blocks.append(((me - step + count) % count, received))
    return blocks


def spread_rows(block):
    other = lax.ppermute(block, "my", [(0, 1), (1, 0)])
    near = lax.ppermute(block, "mc", [(0, 1), (1, 0)])
    return other, near


def rows_in_order(block, other, near):
    my, mc = lax.axis_index("my"), lax.axis_index("mc")
    cores = lax.axis_size("mc")
    far = lax.ppermute(other, "mc", [(0, 1), (1, 0)])
    return [
        (my * cores + mc, block),
        ((1 - my) * cores + mc, other),
        (my * cores + 1 - mc, near),
        ((1 - my) * cores + 1 - mc, far),
    ]


def project_out(attended_full, blocks):
    width = blocks[0][1].shape[0]
    pieces = [
        lax.dynamic_slice_in_dim(attended_full, source * width, width, axis=1)
        for source, unused in blocks
    ]
    weight = jnp.concatenate([block for unused, block in blocks], axis=0)
    return jnp.dot(jnp.concatenate(pieces, axis=1), weight, preferred_element_type=jnp.float32)


def on_device(
    section_input,
    row_code,
    code_table,
    self_gain,
    self_weights,
    self_out,
    cross_gain,
    memory_gain,
    cross_weights,
    cross_out,
):
    local_rows = section_input.shape[1]
    local_width = section_input.shape[2]
    codes_total = code_table.shape[1]
    me = lax.axis_index(MP)
    self_other, self_near = spread_rows(self_out[0])
    cross_blocks = spread(
        lambda target: lax.dynamic_slice_in_dim(cross_out, target * local_width, local_width, axis=1)
    )
    matches = (
        row_code[0][:, None] == lax.broadcasted_iota(jnp.int32, (local_rows, codes_total), 1)
    ).astype(jnp.bfloat16)
    looked = jnp.dot(matches, code_table[0], preferred_element_type=jnp.float32)
    embedded = (section_input[0].astype(jnp.float32) + looked).astype(jnp.bfloat16)
    embedded_full = lax.all_gather(embedded, MP, axis=1, tiled=True)
    normed = rms_norm(embedded_full, self_gain[0])
    self_queries = project(normed, self_weights[0, 0])
    self_pairs = jnp.stack(
        [project(normed, self_weights[0, 1]), project(normed, self_weights[0, 2])]
    )
    self_local, (self_other, self_near, cross_blocks) = attend(
        self_queries, self_pairs, (self_other, self_near, cross_blocks)
    )
    self_blocks = rows_in_order(self_out[0], self_other, self_near)
    self_attended = lax.all_gather(self_local, MP, axis=1, tiled=True)
    hidden_full = (
        embedded_full.astype(jnp.float32) + project_out(self_attended, self_blocks)
    ).astype(jnp.bfloat16)
    hidden_part = lax.dynamic_slice_in_dim(hidden_full, me * local_width, local_width, axis=1)
    cross_queries = project(rms_norm(hidden_full, cross_gain), cross_weights[0])
    memory_normed = rms_norm(hidden_full, memory_gain)
    memory_pairs = jnp.stack(
        [project(memory_normed, cross_weights[1]), project(memory_normed, cross_weights[2])]
    )
    arrived = jnp.stack(
        [shifted(memory_pairs[0], "segment", 1), shifted(memory_pairs[1], "segment", 1)]
    )
    crossed = lax.all_gather(attend(cross_queries, arrived), MP, axis=1, tiled=True)
    decoded = (
        hidden_part.astype(jnp.float32) + project_out(crossed, cross_blocks)
    ).astype(jnp.bfloat16)
    chosen = jnp.where(lax.axis_index("segment") == 0, hidden_part, decoded)
    return chosen[None]


def solution(mesh):
    segments, blocks, parts = (mesh.shape["segment"], mesh.shape["blk"], mesh.shape["mp"])
    split = Mesh(
        mesh.devices.reshape(segments, blocks // X_SIZE, X_SIZE, parts // CORES, CORES),
        ("segment", "bz", "bx", "my", "mc"),
    )
    rows = ("bz", "bx")
    return jax.shard_map(
        on_device,
        mesh=split,
        in_specs=(
            P("segment", rows, MP),
            P("segment", rows),
            P("segment", None, MP),
            P("segment", None),
            P("segment", None, None, MP),
            P("segment", MP, None),
            P(),
            P(),
            P(None, None, MP),
            P(MP, None),
        ),
        out_specs=P("segment", rows, MP),
        check_vma=False,
    )
```

```python
import math

import jax
import jax.numpy as jnp
from jax import lax
from jax.experimental import pallas as pl
from jax.experimental.pallas import tpu as pltpu
from jax.sharding import Mesh
from jax.sharding import PartitionSpec as P

HEAD_DIM = 128
MP = ("my", "mc")
X_SIZE = 4
Z_LO = 2
CORES = 2
TILE = 256
STATS = 128
PARTS = 3


def shifted(value, axis, steps):
    count = lax.axis_size(axis)
    initial, last = (max(0, -steps), min(count, count - steps))
    return lax.ppermute(value, axis, [(source, source + steps) for source in range(initial, last)])


def rms_norm(values, gain):
    widened = values.astype(jnp.float32)
    meansq = jnp.mean(widened * widened, axis=-1, keepdims=True)
    return (widened * lax.rsqrt(meansq + 1e-05) * gain).astype(jnp.bfloat16)


def project(normed, weight):
    return jnp.dot(normed, weight, preferred_element_type=jnp.float32).astype(jnp.bfloat16)


def split_parts(value, count):
    parts = []
    rest = value
    for unused in range(count):
        part = rest.astype(jnp.bfloat16).astype(jnp.float32)
        parts.append(part)
        rest = rest - part
    return parts


def partial_kernel(q_ref, k_ref, v_ref, o_ref):
    heads = q_ref.shape[1] // HEAD_DIM
    rows = q_ref.shape[0]
    lane = lax.broadcasted_iota(jnp.int32, (rows, STATS), 1)
    stats = jnp.zeros((rows, STATS), jnp.float32)
    for h in range(heads):
        cols = slice(h * HEAD_DIM, (h + 1) * HEAD_DIM)
        scores = lax.dot_general(
            q_ref[:, cols], k_ref[:, cols], (((1,), (1,)), ((), ())),
            preferred_element_type=jnp.float32,
        ) * (1.0 / math.sqrt(HEAD_DIM))
        largest = jnp.max(scores, axis=1, keepdims=True)
        weights = jnp.exp(scores - largest)
        summed = jnp.sum(weights, axis=1, keepdims=True)
        o_ref[:, cols] = jnp.dot(
            weights.astype(jnp.bfloat16), v_ref[:, cols], preferred_element_type=jnp.float32
        ).astype(o_ref.dtype)
        for kind, value in enumerate((largest, summed)):
            for piece, part in enumerate(split_parts(value, PARTS)):
                slot = (kind * heads + h) * PARTS + piece
                stats = jnp.where(lane == slot, part, stats)
    o_ref[:, heads * HEAD_DIM:] = stats.astype(o_ref.dtype)


def partial_attend(queries, pairs):
    rows, width = queries.shape
    keys = pairs.shape[1]
    return pl.pallas_call(
        partial_kernel,
        grid=(rows // TILE,),
        in_specs=[
            pl.BlockSpec((TILE, width), lambda i: (i, 0)),
            pl.BlockSpec((None, keys, width), lambda i: (0, 0, 0)),
            pl.BlockSpec((None, keys, width), lambda i: (1, 0, 0)),
        ],
        out_specs=pl.BlockSpec((TILE, width + STATS), lambda i: (i, 0)),
        out_shape=jax.ShapeDtypeStruct((rows, width + STATS), jnp.bfloat16),
        compiler_params=pltpu.CompilerParams(vmem_limit_bytes=48 * 1024 * 1024),
    )(queries, pairs, pairs)


def attend(queries, pairs, riders=None):
    rows, width = queries.shape
    heads = width // HEAD_DIM
    query_block = lax.all_gather(queries, "qa", axis=0, tiled=True)
    key_block = lax.all_gather(pairs, ("kz", "kx"), axis=1, tiled=True)
    partial = partial_attend(query_block, key_block)
    if riders is not None:
        partial, riders = lax.optimization_barrier((partial, riders))
    parts = lax.all_to_all(partial, "qa", 0, 0, tiled=True)
    parts = parts.reshape(-1, rows, width + STATS).astype(jnp.float32)
    outs = parts[:, :, :width].reshape(-1, rows, heads, HEAD_DIM)
    stats = parts[:, :, width:width + 2 * heads * PARTS].reshape(-1, rows, 2, heads, PARTS)
    stats = jnp.sum(stats, axis=-1)
    maxes = stats[:, :, 0]
    sums = stats[:, :, 1]
    top = jnp.max(maxes, axis=0)
    scale = jnp.exp(maxes - top[None])
    total = jnp.sum(sums * scale, axis=0)
    merged = jnp.sum(outs * scale[..., None], axis=0) / total[..., None]
    merged = merged.reshape(rows, width).astype(jnp.bfloat16)
    return merged if riders is None else (merged, riders)


def spread(block_of):
    count = lax.axis_size(MP)
    me = lax.axis_index(MP)
    blocks = [(me, block_of(me))]
    for step in range(1, count):
        piece = block_of((me + step) % count)
        received = lax.ppermute(piece, MP, [(j, (j + step) % count) for j in range(count)])
        blocks.append(((me - step + count) % count, received))
    return blocks


def spread_rows(block):
    other = lax.ppermute(block, "my", [(0, 1), (1, 0)])
    near = lax.ppermute(block, "mc", [(0, 1), (1, 0)])
    return other, near


def rows_in_order(block, other, near):
    my, mc = lax.axis_index("my"), lax.axis_index("mc")
    cores = lax.axis_size("mc")
    far = lax.ppermute(other, "mc", [(0, 1), (1, 0)])
    return [
        (my * cores + mc, block),
        ((1 - my) * cores + mc, other),
        (my * cores + 1 - mc, near),
        ((1 - my) * cores + 1 - mc, far),
    ]


def project_out(attended_full, blocks):
    width = blocks[0][1].shape[0]
    pieces = [
        lax.dynamic_slice_in_dim(attended_full, source * width, width, axis=1)
        for source, unused in blocks
    ]
    weight = jnp.concatenate([block for unused, block in blocks], axis=0)
    return jnp.dot(jnp.concatenate(pieces, axis=1), weight, preferred_element_type=jnp.float32)


def on_device(
    section_input,
    row_code,
    code_table,
    self_gain,
    self_weights,
    self_out,
    cross_gain,
    memory_gain,
    cross_weights,
    cross_out,
):
    local_rows = section_input.shape[1]
    local_width = section_input.shape[2]
    codes_total = code_table.shape[1]
    me = lax.axis_index(MP)
    self_other, self_near = spread_rows(self_out[0])
    cross_blocks = spread(
        lambda target: lax.dynamic_slice_in_dim(cross_out, target * local_width, local_width, axis=1)
    )
    matches = (
        row_code[0][:, None] == lax.broadcasted_iota(jnp.int32, (local_rows, codes_total), 1)
    ).astype(jnp.bfloat16)
    looked = jnp.dot(matches, code_table[0], preferred_element_type=jnp.float32)
    embedded = (section_input[0].astype(jnp.float32) + looked).astype(jnp.bfloat16)
    embedded_full = lax.all_gather(embedded, MP, axis=1, tiled=True)
    normed = rms_norm(embedded_full, self_gain[0])
    self_queries = project(normed, self_weights[0, 0])
    self_pairs = jnp.stack(
        [project(normed, self_weights[0, 1]), project(normed, self_weights[0, 2])]
    )
    self_local, (self_other, self_near, cross_blocks) = attend(
        self_queries, self_pairs, (self_other, self_near, cross_blocks)
    )
    self_blocks = rows_in_order(self_out[0], self_other, self_near)
    self_attended = lax.all_gather(self_local, MP, axis=1, tiled=True)
    hidden_full = (
        embedded_full.astype(jnp.float32) + project_out(self_attended, self_blocks)
    ).astype(jnp.bfloat16)
    hidden_part = lax.dynamic_slice_in_dim(hidden_full, me * local_width, local_width, axis=1)
    cross_queries = project(rms_norm(hidden_full, cross_gain), cross_weights[0])
    memory_normed = rms_norm(hidden_full, memory_gain)
    memory_pairs = jnp.stack(
        [project(memory_normed, cross_weights[1]), project(memory_normed, cross_weights[2])]
    )
    arrived = shifted(memory_pairs, "segment", 1)
    crossed = lax.all_gather(attend(cross_queries, arrived), MP, axis=1, tiled=True)
    decoded = (
        hidden_part.astype(jnp.float32) + project_out(crossed, cross_blocks)
    ).astype(jnp.bfloat16)
    chosen = jnp.where(lax.axis_index("segment") == 0, hidden_part, decoded)
    return chosen[None]


def solution(mesh):
    segments, blocks, parts = (mesh.shape["segment"], mesh.shape["blk"], mesh.shape["mp"])
    split = Mesh(
        mesh.devices.reshape(
            segments, blocks // (Z_LO * X_SIZE), Z_LO, X_SIZE, parts // CORES, CORES
        ),
        ("segment", "qa", "kz", "kx", "my", "mc"),
    )
    rows = ("qa", "kz", "kx")
    return jax.shard_map(
        on_device,
        mesh=split,
        in_specs=(
            P("segment", rows, MP),
            P("segment", rows),
            P("segment", None, MP),
            P("segment", None),
            P("segment", None, None, MP),
            P("segment", MP, None),
            P(),
            P(),
            P(None, None, MP),
            P(MP, None),
        ),
        out_specs=P("segment", rows, MP),
        check_vma=False,
    )
```

```python
import math

import jax
import jax.numpy as jnp
from jax import lax
from jax.experimental import pallas as pl
from jax.experimental.pallas import tpu as pltpu
from jax.sharding import Mesh
from jax.sharding import PartitionSpec as P

HEAD_DIM = 128
MP = ("my", "mc")
X_SIZE = 4
CORES = 2
TILE = 256
STATS = 128
PARTS = 3


def shifted(value, axis, steps):
    count = lax.axis_size(axis)
    initial, last = (max(0, -steps), min(count, count - steps))
    return lax.ppermute(value, axis, [(source, source + steps) for source in range(initial, last)])


def rms_norm(values, gain):
    widened = values.astype(jnp.float32)
    meansq = jnp.mean(widened * widened, axis=-1, keepdims=True)
    return (widened * lax.rsqrt(meansq + 1e-05) * gain).astype(jnp.bfloat16)


def project(normed, weight):
    return jnp.dot(normed, weight, preferred_element_type=jnp.float32).astype(jnp.bfloat16)


def split_parts(value, count):
    parts = []
    rest = value
    for unused in range(count):
        part = rest.astype(jnp.bfloat16).astype(jnp.float32)
        parts.append(part)
        rest = rest - part
    return parts


def partial_kernel(q_ref, k_ref, v_ref, o_ref):
    heads = q_ref.shape[1] // HEAD_DIM
    rows = q_ref.shape[0]
    lane = lax.broadcasted_iota(jnp.int32, (rows, STATS), 1)
    stats = jnp.zeros((rows, STATS), jnp.float32)
    for h in range(heads):
        cols = slice(h * HEAD_DIM, (h + 1) * HEAD_DIM)
        scores = lax.dot_general(
            q_ref[:, cols], k_ref[:, cols], (((1,), (1,)), ((), ())),
            preferred_element_type=jnp.float32,
        ) * (1.0 / math.sqrt(HEAD_DIM))
        largest = jnp.max(scores, axis=1, keepdims=True)
        weights = jnp.exp(scores - largest)
        summed = jnp.sum(weights, axis=1, keepdims=True)
        o_ref[:, cols] = jnp.dot(
            weights.astype(jnp.bfloat16), v_ref[:, cols], preferred_element_type=jnp.float32
        ).astype(o_ref.dtype)
        for kind, value in enumerate((largest, summed)):
            for piece, part in enumerate(split_parts(value, PARTS)):
                slot = (kind * heads + h) * PARTS + piece
                stats = jnp.where(lane == slot, part, stats)
    o_ref[:, heads * HEAD_DIM:] = stats.astype(o_ref.dtype)


def partial_attend(queries, key_block, value_block):
    rows, width = queries.shape
    keys = key_block.shape[0]
    return pl.pallas_call(
        partial_kernel,
        grid=(rows // TILE,),
        in_specs=[
            pl.BlockSpec((TILE, width), lambda i: (i, 0)),
            pl.BlockSpec((keys, width), lambda i: (0, 0)),
            pl.BlockSpec((keys, width), lambda i: (0, 0)),
        ],
        out_specs=pl.BlockSpec((TILE, width + STATS), lambda i: (i, 0)),
        out_shape=jax.ShapeDtypeStruct((rows, width + STATS), jnp.bfloat16),
        compiler_params=pltpu.CompilerParams(vmem_limit_bytes=48 * 1024 * 1024),
    )(queries, key_block, value_block)


def attend(queries, pairs, riders=None):
    rows, width = queries.shape
    heads = width // HEAD_DIM
    query_block = lax.all_gather(queries, "bx", axis=0, tiled=True)
    key_block = lax.all_gather(pairs[0], "bz", axis=0, tiled=True)
    value_block = lax.all_gather(pairs[1], "bz", axis=0, tiled=True)
    partial = partial_attend(query_block, key_block, value_block)
    if riders is not None:
        partial, riders = lax.optimization_barrier((partial, riders))
    parts = lax.all_to_all(partial, "bx", 0, 0, tiled=True)
    parts = parts.reshape(-1, rows, width + STATS).astype(jnp.float32)
    outs = parts[:, :, :width].reshape(-1, rows, heads, HEAD_DIM)
    stats = parts[:, :, width:width + 2 * heads * PARTS].reshape(-1, rows, 2, heads, PARTS)
    stats = jnp.sum(stats, axis=-1)
    maxes = stats[:, :, 0]
    sums = stats[:, :, 1]
    top = jnp.max(maxes, axis=0)
    scale = jnp.exp(maxes - top[None])
    total = jnp.sum(sums * scale, axis=0)
    merged = jnp.sum(outs * scale[..., None], axis=0) / total[..., None]
    merged = merged.reshape(rows, width).astype(jnp.bfloat16)
    return merged if riders is None else (merged, riders)


def spread(block_of):
    count = lax.axis_size(MP)
    me = lax.axis_index(MP)
    blocks = [(me, block_of(me))]
    for step in range(1, count):
        piece = block_of((me + step) % count)
        received = lax.ppermute(piece, MP, [(j, (j + step) % count) for j in range(count)])
        blocks.append(((me - step + count) % count, received))
    return blocks


def spread_rows(block):
    other = lax.ppermute(block, "my", [(0, 1), (1, 0)])
    near = lax.ppermute(block, "mc", [(0, 1), (1, 0)])
    return other, near


def rows_in_order(block, other, near):
    my, mc = lax.axis_index("my"), lax.axis_index("mc")
    cores = lax.axis_size("mc")
    far = lax.ppermute(other, "mc", [(0, 1), (1, 0)])
    return [
        (my * cores + mc, block),
        ((1 - my) * cores + mc, other),
        (my * cores + 1 - mc, near),
        ((1 - my) * cores + 1 - mc, far),
    ]


def project_out(attended_full, blocks):
    width = blocks[0][1].shape[0]
    pieces = [
        lax.dynamic_slice_in_dim(attended_full, source * width, width, axis=1)
        for source, unused in blocks
    ]
    weight = jnp.concatenate([block for unused, block in blocks], axis=0)
    return jnp.dot(jnp.concatenate(pieces, axis=1), weight, preferred_element_type=jnp.float32)


def on_device(
    section_input,
    row_code,
    code_table,
    self_gain,
    self_weights,
    self_out,
    cross_gain,
    memory_gain,
    cross_weights,
    cross_out,
):
    local_rows = section_input.shape[1]
    local_width = section_input.shape[2]
    codes_total = code_table.shape[1]
    me = lax.axis_index(MP)
    self_other, self_near = spread_rows(self_out[0])
    cross_blocks = spread(
        lambda target: lax.dynamic_slice_in_dim(cross_out, target * local_width, local_width, axis=1)
    )
    matches = (
        row_code[0][:, None] == lax.broadcasted_iota(jnp.int32, (local_rows, codes_total), 1)
    ).astype(jnp.bfloat16)
    looked = jnp.dot(matches, code_table[0], preferred_element_type=jnp.float32)
    embedded = (section_input[0].astype(jnp.float32) + looked).astype(jnp.bfloat16)
    embedded_full = lax.all_gather(embedded, MP, axis=1, tiled=True)
    normed = rms_norm(embedded_full, self_gain[0])
    self_queries = project(normed, self_weights[0, 0])
    self_pairs = jnp.stack(
        [project(normed, self_weights[0, 1]), project(normed, self_weights[0, 2])]
    )
    self_local, (self_other, self_near, cross_blocks) = attend(
        self_queries, self_pairs, (self_other, self_near, cross_blocks)
    )
    self_blocks = rows_in_order(self_out[0], self_other, self_near)
    self_attended = lax.all_gather(self_local, MP, axis=1, tiled=True)
    hidden_full = (
        embedded_full.astype(jnp.float32) + project_out(self_attended, self_blocks)
    ).astype(jnp.bfloat16)
    hidden_part = lax.dynamic_slice_in_dim(hidden_full, me * local_width, local_width, axis=1)
    cross_queries = project(rms_norm(hidden_full, cross_gain), cross_weights[0])
    memory_normed = rms_norm(hidden_full, memory_gain)
    memory_pairs = jnp.stack(
        [project(memory_normed, cross_weights[1]), project(memory_normed, cross_weights[2])]
    )
    arrived = shifted(memory_pairs, "segment", 1)
    crossed = lax.all_gather(attend(cross_queries, arrived), MP, axis=1, tiled=True)
    decoded = (
        hidden_part.astype(jnp.float32) + project_out(crossed, cross_blocks)
    ).astype(jnp.bfloat16)
    chosen = jnp.where(lax.axis_index("segment") == 0, hidden_part, decoded)
    return chosen[None]


def solution(mesh):
    segments, blocks, parts = (mesh.shape["segment"], mesh.shape["blk"], mesh.shape["mp"])
    split = Mesh(
        mesh.devices.reshape(segments, blocks // X_SIZE, X_SIZE, parts // CORES, CORES),
        ("segment", "bz", "bx", "my", "mc"),
    )
    rows = ("bz", "bx")
    return jax.shard_map(
        on_device,
        mesh=split,
        in_specs=(
            P("segment", rows, MP),
            P("segment", rows),
            P("segment", None, MP),
            P("segment", None),
            P("segment", None, None, MP),
            P("segment", MP, None),
            P(),
            P(),
            P(None, None, MP),
            P(MP, None),
        ),
        out_specs=P("segment", rows, MP),
        check_vma=False,
    )
```

```python
import math

import jax
import jax.numpy as jnp
from jax import lax
from jax.experimental import pallas as pl
from jax.experimental.pallas import tpu as pltpu
from jax.sharding import Mesh
from jax.sharding import PartitionSpec as P

HEAD_DIM = 128
MP = ("my", "mc")
X_SIZE = 4
CORES = 2
TILE = 256
STATS = 128
PARTS = 3


def shifted(value, axis, steps):
    count = lax.axis_size(axis)
    initial, last = (max(0, -steps), min(count, count - steps))
    return lax.ppermute(value, axis, [(source, source + steps) for source in range(initial, last)])


def rms_norm(values, gain):
    widened = values.astype(jnp.float32)
    meansq = jnp.mean(widened * widened, axis=-1, keepdims=True)
    return (widened * lax.rsqrt(meansq + 1e-05) * gain).astype(jnp.bfloat16)


def project(normed, weight):
    return jnp.dot(normed, weight, preferred_element_type=jnp.float32).astype(jnp.bfloat16)


def split_parts(value, count):
    parts = []
    rest = value
    for unused in range(count):
        part = rest.astype(jnp.bfloat16).astype(jnp.float32)
        parts.append(part)
        rest = rest - part
    return parts


def partial_kernel(q_ref, k_ref, v_ref, o_ref):
    heads = q_ref.shape[1] // HEAD_DIM
    rows = q_ref.shape[0]
    lane = lax.broadcasted_iota(jnp.int32, (rows, STATS), 1)
    stats = jnp.zeros((rows, STATS), jnp.float32)
    for h in range(heads):
        cols = slice(h * HEAD_DIM, (h + 1) * HEAD_DIM)
        scores = lax.dot_general(
            q_ref[:, cols], k_ref[:, cols], (((1,), (1,)), ((), ())),
            preferred_element_type=jnp.float32,
        )
        largest = jnp.max(scores, axis=1, keepdims=True)
        weights = jnp.exp2((scores - largest) * (math.log2(math.e) / math.sqrt(HEAD_DIM)))
        summed = jnp.sum(weights, axis=1, keepdims=True)
        largest = largest * (1.0 / math.sqrt(HEAD_DIM))
        o_ref[:, cols] = jnp.dot(
            weights.astype(jnp.bfloat16), v_ref[:, cols], preferred_element_type=jnp.float32
        ).astype(o_ref.dtype)
        for kind, value in enumerate((largest, summed)):
            for piece, part in enumerate(split_parts(value, PARTS)):
                slot = (kind * heads + h) * PARTS + piece
                stats = jnp.where(lane == slot, part, stats)
    o_ref[:, heads * HEAD_DIM:] = stats.astype(o_ref.dtype)


def partial_attend(queries, pairs):
    rows, width = queries.shape
    keys = pairs.shape[1]
    return pl.pallas_call(
        partial_kernel,
        grid=(rows // TILE,),
        in_specs=[
            pl.BlockSpec((TILE, width), lambda i: (i, 0)),
            pl.BlockSpec((None, keys, width), lambda i: (0, 0, 0)),
            pl.BlockSpec((None, keys, width), lambda i: (1, 0, 0)),
        ],
        out_specs=pl.BlockSpec((TILE, width + STATS), lambda i: (i, 0)),
        out_shape=jax.ShapeDtypeStruct((rows, width + STATS), jnp.bfloat16),
        compiler_params=pltpu.CompilerParams(vmem_limit_bytes=48 * 1024 * 1024),
    )(queries, pairs, pairs)


def attend(queries, pairs, riders=None):
    rows, width = queries.shape
    heads = width // HEAD_DIM
    query_block = lax.all_gather(queries, "bx", axis=0, tiled=True)
    key_block = lax.all_gather(pairs, "bz", axis=1, tiled=True)
    partial = partial_attend(query_block, key_block)
    if riders is not None:
        partial, riders = lax.optimization_barrier((partial, riders))
    parts = lax.all_to_all(partial, "bx", 0, 0, tiled=True)
    parts = parts.reshape(-1, rows, width + STATS).astype(jnp.float32)
    outs = parts[:, :, :width].reshape(-1, rows, heads, HEAD_DIM)
    stats = parts[:, :, width:width + 2 * heads * PARTS].reshape(-1, rows, 2, heads, PARTS)
    stats = jnp.sum(stats, axis=-1)
    maxes = stats[:, :, 0]
    sums = stats[:, :, 1]
    top = jnp.max(maxes, axis=0)
    scale = jnp.exp(maxes - top[None])
    total = jnp.sum(sums * scale, axis=0)
    merged = jnp.sum(outs * scale[..., None], axis=0) / total[..., None]
    merged = merged.reshape(rows, width).astype(jnp.bfloat16)
    return merged if riders is None else (merged, riders)


def spread(block_of):
    count = lax.axis_size(MP)
    me = lax.axis_index(MP)
    blocks = [(me, block_of(me))]
    for step in range(1, count):
        piece = block_of((me + step) % count)
        received = lax.ppermute(piece, MP, [(j, (j + step) % count) for j in range(count)])
        blocks.append(((me - step + count) % count, received))
    return blocks


def spread_rows(block):
    other = lax.ppermute(block, "my", [(0, 1), (1, 0)])
    near = lax.ppermute(block, "mc", [(0, 1), (1, 0)])
    return other, near


def rows_in_order(block, other, near):
    my, mc = lax.axis_index("my"), lax.axis_index("mc")
    cores = lax.axis_size("mc")
    far = lax.ppermute(other, "mc", [(0, 1), (1, 0)])
    return [
        (my * cores + mc, block),
        ((1 - my) * cores + mc, other),
        (my * cores + 1 - mc, near),
        ((1 - my) * cores + 1 - mc, far),
    ]


def project_out(attended_full, blocks):
    width = blocks[0][1].shape[0]
    pieces = [
        lax.dynamic_slice_in_dim(attended_full, source * width, width, axis=1)
        for source, unused in blocks
    ]
    weight = jnp.concatenate([block for unused, block in blocks], axis=0)
    return jnp.dot(jnp.concatenate(pieces, axis=1), weight, preferred_element_type=jnp.float32)


def on_device(
    section_input,
    row_code,
    code_table,
    self_gain,
    self_weights,
    self_out,
    cross_gain,
    memory_gain,
    cross_weights,
    cross_out,
):
    local_rows = section_input.shape[1]
    local_width = section_input.shape[2]
    codes_total = code_table.shape[1]
    me = lax.axis_index(MP)
    self_other, self_near = spread_rows(self_out[0])
    cross_blocks = spread(
        lambda target: lax.dynamic_slice_in_dim(cross_out, target * local_width, local_width, axis=1)
    )
    matches = (
        row_code[0][:, None] == lax.broadcasted_iota(jnp.int32, (local_rows, codes_total), 1)
    ).astype(jnp.bfloat16)
    looked = jnp.dot(matches, code_table[0], preferred_element_type=jnp.float32)
    embedded = (section_input[0].astype(jnp.float32) + looked).astype(jnp.bfloat16)
    embedded_full = lax.all_gather(embedded, MP, axis=1, tiled=True)
    normed = rms_norm(embedded_full, self_gain[0])
    self_queries = project(normed, self_weights[0, 0])
    self_pairs = jnp.stack(
        [project(normed, self_weights[0, 1]), project(normed, self_weights[0, 2])]
    )
    self_local, (self_other, self_near, cross_blocks) = attend(
        self_queries, self_pairs, (self_other, self_near, cross_blocks)
    )
    self_blocks = rows_in_order(self_out[0], self_other, self_near)
    self_attended = lax.all_gather(self_local, MP, axis=1, tiled=True)
    hidden_full = (
        embedded_full.astype(jnp.float32) + project_out(self_attended, self_blocks)
    ).astype(jnp.bfloat16)
    hidden_part = lax.dynamic_slice_in_dim(hidden_full, me * local_width, local_width, axis=1)
    cross_queries = project(rms_norm(hidden_full, cross_gain), cross_weights[0])
    memory_normed = rms_norm(hidden_full, memory_gain)
    memory_pairs = jnp.stack(
        [project(memory_normed, cross_weights[1]), project(memory_normed, cross_weights[2])]
    )
    arrived = shifted(memory_pairs, "segment", 1)
    crossed = lax.all_gather(attend(cross_queries, arrived), MP, axis=1, tiled=True)
    decoded = (
        hidden_part.astype(jnp.float32) + project_out(crossed, cross_blocks)
    ).astype(jnp.bfloat16)
    chosen = jnp.where(lax.axis_index("segment") == 0, hidden_part, decoded)
    return chosen[None]


def solution(mesh):
    segments, blocks, parts = (mesh.shape["segment"], mesh.shape["blk"], mesh.shape["mp"])
    split = Mesh(
        mesh.devices.reshape(segments, blocks // X_SIZE, X_SIZE, parts // CORES, CORES),
        ("segment", "bz", "bx", "my", "mc"),
    )
    rows = ("bz", "bx")
    return jax.shard_map(
        on_device,
        mesh=split,
        in_specs=(
            P("segment", rows, MP),
            P("segment", rows),
            P("segment", None, MP),
            P("segment", None),
            P("segment", None, None, MP),
            P("segment", MP, None),
            P(),
            P(),
            P(None, None, MP),
            P(MP, None),
        ),
        out_specs=P("segment", rows, MP),
        check_vma=False,
    )
```

```python
import math

import jax
import jax.numpy as jnp
from jax import lax
from jax.experimental import pallas as pl
from jax.experimental.pallas import tpu as pltpu
from jax.sharding import Mesh
from jax.sharding import PartitionSpec as P

HEAD_DIM = 128
MP = ("my", "mc")
X_SIZE = 4
CORES = 2
TILE = 512
STATS = 128
PARTS = 3


def shifted(value, axis, steps):
    count = lax.axis_size(axis)
    initial, last = (max(0, -steps), min(count, count - steps))
    return lax.ppermute(value, axis, [(source, source + steps) for source in range(initial, last)])


def rms_norm(values, gain):
    widened = values.astype(jnp.float32)
    meansq = jnp.mean(widened * widened, axis=-1, keepdims=True)
    return (widened * lax.rsqrt(meansq + 1e-05) * gain).astype(jnp.bfloat16)


def project(normed, weight):
    return jnp.dot(normed, weight, preferred_element_type=jnp.float32).astype(jnp.bfloat16)


def split_parts(value, count):
    parts = []
    rest = value
    for unused in range(count):
        part = rest.astype(jnp.bfloat16).astype(jnp.float32)
        parts.append(part)
        rest = rest - part
    return parts


def partial_kernel(q_ref, k_ref, v_ref, o_ref):
    heads = q_ref.shape[1] // HEAD_DIM
    rows = q_ref.shape[0]
    lane = lax.broadcasted_iota(jnp.int32, (rows, STATS), 1)
    stats = jnp.zeros((rows, STATS), jnp.float32)
    for h in range(heads):
        cols = slice(h * HEAD_DIM, (h + 1) * HEAD_DIM)
        scores = lax.dot_general(
            q_ref[:, cols], k_ref[:, cols], (((1,), (1,)), ((), ())),
            preferred_element_type=jnp.float32,
        )
        largest = jnp.max(scores, axis=1, keepdims=True)
        weights = jnp.exp2((scores - largest) * (math.log2(math.e) / math.sqrt(HEAD_DIM)))
        summed = jnp.sum(weights, axis=1, keepdims=True)
        largest = largest * (1.0 / math.sqrt(HEAD_DIM))
        o_ref[:, cols] = jnp.dot(
            weights.astype(jnp.bfloat16), v_ref[:, cols], preferred_element_type=jnp.float32
        ).astype(o_ref.dtype)
        for kind, value in enumerate((largest, summed)):
            for piece, part in enumerate(split_parts(value, PARTS)):
                slot = (kind * heads + h) * PARTS + piece
                stats = jnp.where(lane == slot, part, stats)
    o_ref[:, heads * HEAD_DIM:] = stats.astype(o_ref.dtype)


def partial_attend(queries, pairs):
    rows, width = queries.shape
    keys = pairs.shape[1]
    return pl.pallas_call(
        partial_kernel,
        grid=(rows // TILE,),
        in_specs=[
            pl.BlockSpec((TILE, width), lambda i: (i, 0)),
            pl.BlockSpec((None, keys, width), lambda i: (0, 0, 0)),
            pl.BlockSpec((None, keys, width), lambda i: (1, 0, 0)),
        ],
        out_specs=pl.BlockSpec((TILE, width + STATS), lambda i: (i, 0)),
        out_shape=jax.ShapeDtypeStruct((rows, width + STATS), jnp.bfloat16),
        compiler_params=pltpu.CompilerParams(vmem_limit_bytes=48 * 1024 * 1024),
    )(queries, pairs, pairs)


def attend(queries, pairs, riders=None):
    rows, width = queries.shape
    heads = width // HEAD_DIM
    query_block = lax.all_gather(queries, "bx", axis=0, tiled=True)
    key_block = lax.all_gather(pairs, "bz", axis=1, tiled=True)
    partial = partial_attend(query_block, key_block)
    if riders is not None:
        partial, riders = lax.optimization_barrier((partial, riders))
    parts = lax.all_to_all(partial, "bx", 0, 0, tiled=True)
    parts = parts.reshape(-1, rows, width + STATS).astype(jnp.float32)
    outs = parts[:, :, :width].reshape(-1, rows, heads, HEAD_DIM)
    stats = parts[:, :, width:width + 2 * heads * PARTS].reshape(-1, rows, 2, heads, PARTS)
    stats = jnp.sum(stats, axis=-1)
    maxes = stats[:, :, 0]
    sums = stats[:, :, 1]
    top = jnp.max(maxes, axis=0)
    scale = jnp.exp(maxes - top[None])
    total = jnp.sum(sums * scale, axis=0)
    merged = jnp.sum(outs * scale[..., None], axis=0) / total[..., None]
    merged = merged.reshape(rows, width).astype(jnp.bfloat16)
    return merged if riders is None else (merged, riders)


def spread(block_of):
    count = lax.axis_size(MP)
    me = lax.axis_index(MP)
    blocks = [(me, block_of(me))]
    for step in range(1, count):
        piece = block_of((me + step) % count)
        received = lax.ppermute(piece, MP, [(j, (j + step) % count) for j in range(count)])
        blocks.append(((me - step + count) % count, received))
    return blocks


def spread_rows(block):
    other = lax.ppermute(block, "my", [(0, 1), (1, 0)])
    near = lax.ppermute(block, "mc", [(0, 1), (1, 0)])
    return other, near


def rows_in_order(block, other, near):
    my, mc = lax.axis_index("my"), lax.axis_index("mc")
    cores = lax.axis_size("mc")
    far = lax.ppermute(other, "mc", [(0, 1), (1, 0)])
    return [
        (my * cores + mc, block),
        ((1 - my) * cores + mc, other),
        (my * cores + 1 - mc, near),
        ((1 - my) * cores + 1 - mc, far),
    ]


def project_out(attended_full, blocks):
    width = blocks[0][1].shape[0]
    pieces = [
        lax.dynamic_slice_in_dim(attended_full, source * width, width, axis=1)
        for source, unused in blocks
    ]
    weight = jnp.concatenate([block for unused, block in blocks], axis=0)
    return jnp.dot(jnp.concatenate(pieces, axis=1), weight, preferred_element_type=jnp.float32)


def on_device(
    section_input,
    row_code,
    code_table,
    self_gain,
    self_weights,
    self_out,
    cross_gain,
    memory_gain,
    cross_weights,
    cross_out,
):
    local_rows = section_input.shape[1]
    local_width = section_input.shape[2]
    codes_total = code_table.shape[1]
    me = lax.axis_index(MP)
    self_other, self_near = spread_rows(self_out[0])
    cross_blocks = spread(
        lambda target: lax.dynamic_slice_in_dim(cross_out, target * local_width, local_width, axis=1)
    )
    matches = (
        row_code[0][:, None] == lax.broadcasted_iota(jnp.int32, (local_rows, codes_total), 1)
    ).astype(jnp.bfloat16)
    looked = jnp.dot(matches, code_table[0], preferred_element_type=jnp.float32)
    embedded = (section_input[0].astype(jnp.float32) + looked).astype(jnp.bfloat16)
    embedded_full = lax.all_gather(embedded, MP, axis=1, tiled=True)
    normed = rms_norm(embedded_full, self_gain[0])
    self_queries = project(normed, self_weights[0, 0])
    self_pairs = jnp.stack(
        [project(normed, self_weights[0, 1]), project(normed, self_weights[0, 2])]
    )
    self_local, (self_other, self_near, cross_blocks) = attend(
        self_queries, self_pairs, (self_other, self_near, cross_blocks)
    )
    self_blocks = rows_in_order(self_out[0], self_other, self_near)
    self_attended = lax.all_gather(self_local, MP, axis=1, tiled=True)
    hidden_full = (
        embedded_full.astype(jnp.float32) + project_out(self_attended, self_blocks)
    ).astype(jnp.bfloat16)
    hidden_part = lax.dynamic_slice_in_dim(hidden_full, me * local_width, local_width, axis=1)
    cross_queries = project(rms_norm(hidden_full, cross_gain), cross_weights[0])
    memory_normed = rms_norm(hidden_full, memory_gain)
    memory_pairs = jnp.stack(
        [project(memory_normed, cross_weights[1]), project(memory_normed, cross_weights[2])]
    )
    arrived = shifted(memory_pairs, "segment", 1)
    crossed = lax.all_gather(attend(cross_queries, arrived), MP, axis=1, tiled=True)
    decoded = (
        hidden_part.astype(jnp.float32) + project_out(crossed, cross_blocks)
    ).astype(jnp.bfloat16)
    chosen = jnp.where(lax.axis_index("segment") == 0, hidden_part, decoded)
    return chosen[None]


def solution(mesh):
    segments, blocks, parts = (mesh.shape["segment"], mesh.shape["blk"], mesh.shape["mp"])
    split = Mesh(
        mesh.devices.reshape(segments, blocks // X_SIZE, X_SIZE, parts // CORES, CORES),
        ("segment", "bz", "bx", "my", "mc"),
    )
    rows = ("bz", "bx")
    return jax.shard_map(
        on_device,
        mesh=split,
        in_specs=(
            P("segment", rows, MP),
            P("segment", rows),
            P("segment", None, MP),
            P("segment", None),
            P("segment", None, None, MP),
            P("segment", MP, None),
            P(),
            P(),
            P(None, None, MP),
            P(MP, None),
        ),
        out_specs=P("segment", rows, MP),
        check_vma=False,
    )
```

```python
import math

import jax
import jax.numpy as jnp
from jax import lax
from jax.experimental import pallas as pl
from jax.experimental.pallas import tpu as pltpu
from jax.sharding import Mesh
from jax.sharding import PartitionSpec as P

HEAD_DIM = 128
MP = ("my", "mc")
X_SIZE = 4
CORES = 2
TILE = 256
STATS = 128
PARTS = 3


def shifted(value, axis, steps):
    count = lax.axis_size(axis)
    initial, last = (max(0, -steps), min(count, count - steps))
    return lax.ppermute(value, axis, [(source, source + steps) for source in range(initial, last)])


def rms_norm(values, gain):
    widened = values.astype(jnp.float32)
    meansq = jnp.mean(widened * widened, axis=-1, keepdims=True)
    return (widened * lax.rsqrt(meansq + 1e-05) * gain).astype(jnp.bfloat16)


def project(normed, weight):
    return jnp.dot(normed, weight, preferred_element_type=jnp.float32).astype(jnp.bfloat16)


def split_parts(value, count):
    parts = []
    rest = value
    for unused in range(count):
        part = rest.astype(jnp.bfloat16).astype(jnp.float32)
        parts.append(part)
        rest = rest - part
    return parts


def partial_kernel(q_ref, k_ref, v_ref, o_ref):
    heads = q_ref.shape[1] // HEAD_DIM
    rows = q_ref.shape[0]
    lane = lax.broadcasted_iota(jnp.int32, (rows, STATS), 1)
    stats = jnp.zeros((rows, STATS), jnp.float32)
    for h in range(heads):
        cols = slice(h * HEAD_DIM, (h + 1) * HEAD_DIM)
        scores = lax.dot_general(
            q_ref[:, cols], k_ref[:, cols], (((1,), (1,)), ((), ())),
            preferred_element_type=jnp.float32,
        )
        largest = jnp.max(scores, axis=1, keepdims=True)
        weights = jnp.exp2((scores - largest) * (math.log2(math.e) / math.sqrt(HEAD_DIM)))
        summed = jnp.sum(weights, axis=1, keepdims=True)
        largest = largest * (1.0 / math.sqrt(HEAD_DIM))
        o_ref[:, cols] = jnp.dot(
            weights.astype(jnp.bfloat16), v_ref[:, cols], preferred_element_type=jnp.float32
        ).astype(o_ref.dtype)
        for kind, value in enumerate((largest, summed)):
            for piece, part in enumerate(split_parts(value, PARTS)):
                slot = (kind * heads + h) * PARTS + piece
                stats = jnp.where(lane == slot, part, stats)
    o_ref[:, heads * HEAD_DIM:] = stats.astype(o_ref.dtype)


def partial_attend(queries, pairs):
    rows, width = queries.shape
    keys = pairs.shape[1]
    return pl.pallas_call(
        partial_kernel,
        grid=(rows // TILE,),
        in_specs=[
            pl.BlockSpec((TILE, width), lambda i: (i, 0)),
            pl.BlockSpec((None, keys, width), lambda i: (0, 0, 0)),
            pl.BlockSpec((None, keys, width), lambda i: (1, 0, 0)),
        ],
        out_specs=pl.BlockSpec((TILE, width + STATS), lambda i: (i, 0)),
        out_shape=jax.ShapeDtypeStruct((rows, width + STATS), jnp.bfloat16),
        compiler_params=pltpu.CompilerParams(vmem_limit_bytes=48 * 1024 * 1024),
    )(queries, pairs, pairs)


def attend(queries, pairs, riders=None):
    rows, width = queries.shape
    heads = width // HEAD_DIM
    query_block = lax.all_gather(queries, "bx", axis=0, tiled=True)
    key_block = lax.all_gather(pairs, "bz", axis=1, tiled=True)
    partial = partial_attend(query_block, key_block)
    if riders is not None:
        partial, riders = lax.optimization_barrier((partial, riders))
    parts = lax.all_to_all(partial, "bx", 0, 0, tiled=True)
    parts = parts.reshape(-1, rows, width + STATS).astype(jnp.float32)
    outs = parts[:, :, :width].reshape(-1, rows, heads, HEAD_DIM)
    stats = parts[:, :, width:width + 2 * heads * PARTS].reshape(-1, rows, 2, heads, PARTS)
    stats = jnp.sum(stats, axis=-1)
    maxes = stats[:, :, 0]
    sums = stats[:, :, 1]
    top = jnp.max(maxes, axis=0)
    scale = jnp.exp(maxes - top[None])
    total = jnp.sum(sums * scale, axis=0)
    merged = jnp.sum(outs * scale[..., None], axis=0) / total[..., None]
    merged = merged.reshape(rows, width).astype(jnp.bfloat16)
    return merged if riders is None else (merged, riders)


def spread(block_of):
    count = lax.axis_size(MP)
    me = lax.axis_index(MP)
    blocks = [(me, block_of(me))]
    for step in range(1, count):
        piece = block_of((me + step) % count)
        received = lax.ppermute(piece, MP, [(j, (j + step) % count) for j in range(count)])
        blocks.append(((me - step + count) % count, received))
    return blocks


def spread_rows(block):
    other = lax.ppermute(block, "my", [(0, 1), (1, 0)])
    near = lax.ppermute(block, "mc", [(0, 1), (1, 0)])
    return other, near


def rows_in_order(block, other, near):
    my, mc = lax.axis_index("my"), lax.axis_index("mc")
    cores = lax.axis_size("mc")
    far = lax.ppermute(other, "mc", [(0, 1), (1, 0)])
    return [
        (my * cores + mc, block),
        ((1 - my) * cores + mc, other),
        (my * cores + 1 - mc, near),
        ((1 - my) * cores + 1 - mc, far),
    ]


def mp_gather_flat(value):
    return lax.all_gather(value, MP, axis=1, tiled=True)


def project_out(attended_full, blocks):
    width = blocks[0][1].shape[0]
    pieces = [
        lax.dynamic_slice_in_dim(attended_full, source * width, width, axis=1)
        for source, unused in blocks
    ]
    weight = jnp.concatenate([block for unused, block in blocks], axis=0)
    return jnp.dot(jnp.concatenate(pieces, axis=1), weight, preferred_element_type=jnp.float32)


def on_device(
    section_input,
    row_code,
    code_table,
    self_gain,
    self_weights,
    self_out,
    cross_gain,
    memory_gain,
    cross_weights,
    cross_out,
):
    local_rows = section_input.shape[1]
    local_width = section_input.shape[2]
    codes_total = code_table.shape[1]
    me = lax.axis_index(MP)
    self_other, self_near = spread_rows(self_out[0])
    cross_blocks = spread(
        lambda target: lax.dynamic_slice_in_dim(cross_out, target * local_width, local_width, axis=1)
    )
    matches = (
        row_code[0][:, None] == lax.broadcasted_iota(jnp.int32, (local_rows, codes_total), 1)
    ).astype(jnp.bfloat16)
    looked = jnp.dot(matches, code_table[0], preferred_element_type=jnp.float32)
    embedded = (section_input[0].astype(jnp.float32) + looked).astype(jnp.bfloat16)
    embedded_full = lax.all_gather(embedded, MP, axis=1, tiled=True)
    normed = rms_norm(embedded_full, self_gain[0])
    self_queries = project(normed, self_weights[0, 0])
    self_pairs = jnp.stack(
        [project(normed, self_weights[0, 1]), project(normed, self_weights[0, 2])]
    )
    self_local, (self_other, self_near, cross_blocks) = attend(
        self_queries, self_pairs, (self_other, self_near, cross_blocks)
    )
    self_blocks = rows_in_order(self_out[0], self_other, self_near)
    self_attended = lax.all_gather(self_local, MP, axis=1, tiled=True)
    hidden_full = (
        embedded_full.astype(jnp.float32) + project_out(self_attended, self_blocks)
    ).astype(jnp.bfloat16)
    hidden_part = lax.dynamic_slice_in_dim(hidden_full, me * local_width, local_width, axis=1)
    cross_queries = project(rms_norm(hidden_full, cross_gain), cross_weights[0])
    memory_normed = rms_norm(hidden_full, memory_gain)
    memory_pairs = jnp.stack(
        [project(memory_normed, cross_weights[1]), project(memory_normed, cross_weights[2])]
    )
    voxel_queries = shifted(cross_queries, "segment", -1)
    voxel_part = shifted(hidden_part, "segment", -1)
    crossed = mp_gather_flat(attend(voxel_queries, memory_pairs))
    decoded = (
        voxel_part.astype(jnp.float32) + project_out(crossed, cross_blocks)
    ).astype(jnp.bfloat16)
    returned = shifted(decoded, "segment", 1)
    chosen = jnp.where(lax.axis_index("segment") == 0, hidden_part, returned)
    return chosen[None]


def solution(mesh):
    segments, blocks, parts = (mesh.shape["segment"], mesh.shape["blk"], mesh.shape["mp"])
    split = Mesh(
        mesh.devices.reshape(segments, blocks // X_SIZE, X_SIZE, parts // CORES, CORES),
        ("segment", "bz", "bx", "my", "mc"),
    )
    rows = ("bz", "bx")
    return jax.shard_map(
        on_device,
        mesh=split,
        in_specs=(
            P("segment", rows, MP),
            P("segment", rows),
            P("segment", None, MP),
            P("segment", None),
            P("segment", None, None, MP),
            P("segment", MP, None),
            P(),
            P(),
            P(None, None, MP),
            P(MP, None),
        ),
        out_specs=P("segment", rows, MP),
        check_vma=False,
    )
```

```python
import math

import jax
import jax.numpy as jnp
from jax import lax
from jax.experimental import pallas as pl
from jax.experimental.pallas import tpu as pltpu
from jax.sharding import Mesh
from jax.sharding import PartitionSpec as P

HEAD_DIM = 128
MP = ("my", "mc")
X_SIZE = 4
CORES = 2
TILE = 256
STATS = 128
PARTS = 3


def shifted(value, axis, steps):
    count = lax.axis_size(axis)
    initial, last = (max(0, -steps), min(count, count - steps))
    return lax.ppermute(value, axis, [(source, source + steps) for source in range(initial, last)])


def rms_norm(values, gain):
    widened = values.astype(jnp.float32)
    meansq = jnp.mean(widened * widened, axis=-1, keepdims=True)
    return (widened * lax.rsqrt(meansq + 1e-05) * gain).astype(jnp.bfloat16)


def project(normed, weight):
    return jnp.dot(normed, weight, preferred_element_type=jnp.float32).astype(jnp.bfloat16)


def split_parts(value, count):
    parts = []
    rest = value
    for unused in range(count):
        part = rest.astype(jnp.bfloat16).astype(jnp.float32)
        parts.append(part)
        rest = rest - part
    return parts


def partial_kernel(q_ref, k_ref, v_ref, o_ref):
    heads = q_ref.shape[1] // HEAD_DIM
    rows = q_ref.shape[0]
    lane = lax.broadcasted_iota(jnp.int32, (rows, STATS), 1)
    stats = jnp.zeros((rows, STATS), jnp.float32)
    for h in range(heads):
        cols = slice(h * HEAD_DIM, (h + 1) * HEAD_DIM)
        scores = lax.dot_general(
            q_ref[:, cols], k_ref[:, cols], (((1,), (1,)), ((), ())),
            preferred_element_type=jnp.float32,
        )
        largest = jnp.max(scores, axis=1, keepdims=True)
        weights = jnp.exp2((scores - largest) * (math.log2(math.e) / math.sqrt(HEAD_DIM)))
        summed = jnp.sum(weights, axis=1, keepdims=True)
        largest = largest * (1.0 / math.sqrt(HEAD_DIM))
        o_ref[:, cols] = jnp.dot(
            weights.astype(jnp.bfloat16), v_ref[:, cols], preferred_element_type=jnp.float32
        ).astype(o_ref.dtype)
        for kind, value in enumerate((largest, summed)):
            for piece, part in enumerate(split_parts(value, PARTS)):
                slot = (kind * heads + h) * PARTS + piece
                stats = jnp.where(lane == slot, part, stats)
    o_ref[:, heads * HEAD_DIM:] = stats.astype(o_ref.dtype)


def partial_attend(queries, pairs):
    rows, width = queries.shape
    keys = pairs.shape[1]
    return pl.pallas_call(
        partial_kernel,
        grid=(rows // TILE,),
        in_specs=[
            pl.BlockSpec((TILE, width), lambda i: (i, 0)),
            pl.BlockSpec((None, keys, width), lambda i: (0, 0, 0)),
            pl.BlockSpec((None, keys, width), lambda i: (1, 0, 0)),
        ],
        out_specs=pl.BlockSpec((TILE, width + STATS), lambda i: (i, 0)),
        out_shape=jax.ShapeDtypeStruct((rows, width + STATS), jnp.bfloat16),
        compiler_params=pltpu.CompilerParams(vmem_limit_bytes=48 * 1024 * 1024),
    )(queries, pairs, pairs)


def attend(queries, pairs, riders=None, by_permutes=False):
    rows, width = queries.shape
    heads = width // HEAD_DIM
    query_block = lax.all_gather(queries, "bx", axis=0, tiled=True)
    key_block = lax.all_gather(pairs, "bz", axis=1, tiled=True)
    partial = partial_attend(query_block, key_block)
    if riders is not None:
        partial, riders = lax.optimization_barrier((partial, riders))
    if by_permutes:
        count = lax.axis_size("bx")
        me = lax.axis_index("bx")
        chunks = [lax.dynamic_slice_in_dim(partial, me * rows, rows, axis=0)]
        for step in range(1, count):
            piece = lax.dynamic_slice_in_dim(partial, ((me + step) % count) * rows, rows, axis=0)
            chunks.append(
                lax.ppermute(piece, "bx", [(j, (j + step) % count) for j in range(count)])
            )
        parts = jnp.stack(chunks)
    else:
        parts = lax.all_to_all(partial, "bx", 0, 0, tiled=True)
    parts = parts.reshape(-1, rows, width + STATS).astype(jnp.float32)
    outs = parts[:, :, :width].reshape(-1, rows, heads, HEAD_DIM)
    stats = parts[:, :, width:width + 2 * heads * PARTS].reshape(-1, rows, 2, heads, PARTS)
    stats = jnp.sum(stats, axis=-1)
    maxes = stats[:, :, 0]
    sums = stats[:, :, 1]
    top = jnp.max(maxes, axis=0)
    scale = jnp.exp(maxes - top[None])
    total = jnp.sum(sums * scale, axis=0)
    merged = jnp.sum(outs * scale[..., None], axis=0) / total[..., None]
    merged = merged.reshape(rows, width).astype(jnp.bfloat16)
    return merged if riders is None else (merged, riders)


def spread(block_of):
    count = lax.axis_size(MP)
    me = lax.axis_index(MP)
    blocks = [(me, block_of(me))]
    for step in range(1, count):
        piece = block_of((me + step) % count)
        received = lax.ppermute(piece, MP, [(j, (j + step) % count) for j in range(count)])
        blocks.append(((me - step + count) % count, received))
    return blocks


def spread_rows(block):
    other = lax.ppermute(block, "my", [(0, 1), (1, 0)])
    near = lax.ppermute(block, "mc", [(0, 1), (1, 0)])
    return other, near


def rows_in_order(block, other, near):
    my, mc = lax.axis_index("my"), lax.axis_index("mc")
    cores = lax.axis_size("mc")
    far = lax.ppermute(other, "mc", [(0, 1), (1, 0)])
    return [
        (my * cores + mc, block),
        ((1 - my) * cores + mc, other),
        (my * cores + 1 - mc, near),
        ((1 - my) * cores + 1 - mc, far),
    ]


def mp_gather_flat(value):
    return lax.all_gather(value, MP, axis=1, tiled=True)


def project_out(attended_full, blocks):
    width = blocks[0][1].shape[0]
    pieces = [
        lax.dynamic_slice_in_dim(attended_full, source * width, width, axis=1)
        for source, unused in blocks
    ]
    weight = jnp.concatenate([block for unused, block in blocks], axis=0)
    return jnp.dot(jnp.concatenate(pieces, axis=1), weight, preferred_element_type=jnp.float32)


def on_device(
    section_input,
    row_code,
    code_table,
    self_gain,
    self_weights,
    self_out,
    cross_gain,
    memory_gain,
    cross_weights,
    cross_out,
):
    local_rows = section_input.shape[1]
    local_width = section_input.shape[2]
    codes_total = code_table.shape[1]
    me = lax.axis_index(MP)
    self_other, self_near = spread_rows(self_out[0])
    cross_blocks = spread(
        lambda target: lax.dynamic_slice_in_dim(cross_out, target * local_width, local_width, axis=1)
    )
    matches = (
        row_code[0][:, None] == lax.broadcasted_iota(jnp.int32, (local_rows, codes_total), 1)
    ).astype(jnp.bfloat16)
    looked = jnp.dot(matches, code_table[0], preferred_element_type=jnp.float32)
    embedded = (section_input[0].astype(jnp.float32) + looked).astype(jnp.bfloat16)
    embedded_full = lax.all_gather(embedded, MP, axis=1, tiled=True)
    normed = rms_norm(embedded_full, self_gain[0])
    self_queries = project(normed, self_weights[0, 0])
    self_pairs = jnp.stack(
        [project(normed, self_weights[0, 1]), project(normed, self_weights[0, 2])]
    )
    self_local, (self_other, self_near, cross_blocks) = attend(
        self_queries, self_pairs, (self_other, self_near, cross_blocks), by_permutes=True
    )
    self_blocks = rows_in_order(self_out[0], self_other, self_near)
    self_attended = lax.all_gather(self_local, MP, axis=1, tiled=True)
    hidden_full = (
        embedded_full.astype(jnp.float32) + project_out(self_attended, self_blocks)
    ).astype(jnp.bfloat16)
    hidden_part = lax.dynamic_slice_in_dim(hidden_full, me * local_width, local_width, axis=1)
    cross_queries = project(rms_norm(hidden_full, cross_gain), cross_weights[0])
    memory_normed = rms_norm(hidden_full, memory_gain)
    memory_pairs = jnp.stack(
        [project(memory_normed, cross_weights[1]), project(memory_normed, cross_weights[2])]
    )
    voxel_queries = shifted(cross_queries, "segment", -1)
    voxel_part = shifted(hidden_part, "segment", -1)
    crossed = mp_gather_flat(attend(voxel_queries, memory_pairs))
    decoded = (
        voxel_part.astype(jnp.float32) + project_out(crossed, cross_blocks)
    ).astype(jnp.bfloat16)
    returned = shifted(decoded, "segment", 1)
    chosen = jnp.where(lax.axis_index("segment") == 0, hidden_part, returned)
    return chosen[None]


def solution(mesh):
    segments, blocks, parts = (mesh.shape["segment"], mesh.shape["blk"], mesh.shape["mp"])
    split = Mesh(
        mesh.devices.reshape(segments, blocks // X_SIZE, X_SIZE, parts // CORES, CORES),
        ("segment", "bz", "bx", "my", "mc"),
    )
    rows = ("bz", "bx")
    return jax.shard_map(
        on_device,
        mesh=split,
        in_specs=(
            P("segment", rows, MP),
            P("segment", rows),
            P("segment", None, MP),
            P("segment", None),
            P("segment", None, None, MP),
            P("segment", MP, None),
            P(),
            P(),
            P(None, None, MP),
            P(MP, None),
        ),
        out_specs=P("segment", rows, MP),
        check_vma=False,
    )
```

```python
import math

import jax
import jax.numpy as jnp
from jax import lax
from jax.experimental import pallas as pl
from jax.experimental.pallas import tpu as pltpu
from jax.sharding import Mesh
from jax.sharding import PartitionSpec as P

HEAD_DIM = 128
MP = ("my", "mc")
X_SIZE = 4
CORES = 2
TILE = 256
STATS = 128
PARTS = 3


def shifted(value, axis, steps):
    count = lax.axis_size(axis)
    initial, last = (max(0, -steps), min(count, count - steps))
    return lax.ppermute(value, axis, [(source, source + steps) for source in range(initial, last)])


def rms_norm(values, gain):
    widened = values.astype(jnp.float32)
    meansq = jnp.mean(widened * widened, axis=-1, keepdims=True)
    return (widened * lax.rsqrt(meansq + 1e-05) * gain).astype(jnp.bfloat16)


def project(normed, weight):
    return jnp.dot(normed, weight, preferred_element_type=jnp.float32).astype(jnp.bfloat16)


def split_parts(value, count):
    parts = []
    rest = value
    for unused in range(count):
        part = rest.astype(jnp.bfloat16).astype(jnp.float32)
        parts.append(part)
        rest = rest - part
    return parts


def partial_kernel(q_ref, k_ref, v_ref, o_ref):
    heads = q_ref.shape[1] // HEAD_DIM
    rows = q_ref.shape[0]
    lane = lax.broadcasted_iota(jnp.int32, (rows, STATS), 1)
    stats = jnp.zeros((rows, STATS), jnp.float32)
    for h in range(heads):
        cols = slice(h * HEAD_DIM, (h + 1) * HEAD_DIM)
        scores = lax.dot_general(
            q_ref[:, cols], k_ref[:, cols], (((1,), (1,)), ((), ())),
            preferred_element_type=jnp.float32,
        )
        largest = jnp.max(scores, axis=1, keepdims=True)
        weights = jnp.exp2((scores - largest) * (math.log2(math.e) / math.sqrt(HEAD_DIM)))
        summed = jnp.sum(weights, axis=1, keepdims=True)
        largest = largest * (1.0 / math.sqrt(HEAD_DIM))
        o_ref[:, cols] = jnp.dot(
            weights.astype(jnp.bfloat16), v_ref[:, cols], preferred_element_type=jnp.float32
        ).astype(o_ref.dtype)
        for kind, value in enumerate((largest, summed)):
            for piece, part in enumerate(split_parts(value, PARTS)):
                slot = (kind * heads + h) * PARTS + piece
                stats = jnp.where(lane == slot, part, stats)
    o_ref[:, heads * HEAD_DIM:] = stats.astype(o_ref.dtype)


def partial_attend(queries, pairs):
    rows, width = queries.shape
    keys = pairs.shape[1]
    return pl.pallas_call(
        partial_kernel,
        grid=(rows // TILE,),
        in_specs=[
            pl.BlockSpec((TILE, width), lambda i: (i, 0)),
            pl.BlockSpec((None, keys, width), lambda i: (0, 0, 0)),
            pl.BlockSpec((None, keys, width), lambda i: (1, 0, 0)),
        ],
        out_specs=pl.BlockSpec((TILE, width + STATS), lambda i: (i, 0)),
        out_shape=jax.ShapeDtypeStruct((rows, width + STATS), jnp.bfloat16),
        compiler_params=pltpu.CompilerParams(vmem_limit_bytes=48 * 1024 * 1024),
    )(queries, pairs, pairs)


def attend(queries, pairs, riders=None, by_permutes=False):
    rows, width = queries.shape
    heads = width // HEAD_DIM
    query_block = lax.all_gather(queries, "bx", axis=0, tiled=True)
    key_block = lax.all_gather(pairs, "bz", axis=1, tiled=True)
    partial = partial_attend(query_block, key_block)
    if riders is not None:
        partial, riders = lax.optimization_barrier((partial, riders))
    if by_permutes:
        count = lax.axis_size("bx")
        me = lax.axis_index("bx")
        chunks = [lax.dynamic_slice_in_dim(partial, me * rows, rows, axis=0)]
        for step in range(1, count):
            piece = lax.dynamic_slice_in_dim(partial, ((me + step) % count) * rows, rows, axis=0)
            chunks.append(
                lax.ppermute(piece, "bx", [(j, (j + step) % count) for j in range(count)])
            )
        parts = jnp.stack(chunks)
    else:
        parts = lax.all_to_all(partial, "bx", 0, 0, tiled=True)
    parts = parts.reshape(-1, rows, width + STATS).astype(jnp.float32)
    outs = parts[:, :, :width].reshape(-1, rows, heads, HEAD_DIM)
    stats = parts[:, :, width:width + 2 * heads * PARTS].reshape(-1, rows, 2, heads, PARTS)
    stats = jnp.sum(stats, axis=-1)
    maxes = stats[:, :, 0]
    sums = stats[:, :, 1]
    top = jnp.max(maxes, axis=0)
    scale = jnp.exp(maxes - top[None])
    total = jnp.sum(sums * scale, axis=0)
    merged = jnp.sum(outs * scale[..., None], axis=0) / total[..., None]
    merged = merged.reshape(rows, width).astype(jnp.bfloat16)
    return merged if riders is None else (merged, riders)


def spread(block_of):
    count = lax.axis_size(MP)
    me = lax.axis_index(MP)
    blocks = [(me, block_of(me))]
    for step in range(1, count):
        piece = block_of((me + step) % count)
        received = lax.ppermute(piece, MP, [(j, (j + step) % count) for j in range(count)])
        blocks.append(((me - step + count) % count, received))
    return blocks


def spread_rows(block):
    other = lax.ppermute(block, "my", [(0, 1), (1, 0)])
    near = lax.ppermute(block, "mc", [(0, 1), (1, 0)])
    return other, near


def rows_in_order(block, other, near):
    my, mc = lax.axis_index("my"), lax.axis_index("mc")
    cores = lax.axis_size("mc")
    far = lax.ppermute(other, "mc", [(0, 1), (1, 0)])
    return [
        (my * cores + mc, block),
        ((1 - my) * cores + mc, other),
        (my * cores + 1 - mc, near),
        ((1 - my) * cores + 1 - mc, far),
    ]


def mp_gather_flat(value):
    return lax.all_gather(value, MP, axis=1, tiled=True)


def project_out(attended_full, blocks):
    width = blocks[0][1].shape[0]
    pieces = [
        lax.dynamic_slice_in_dim(attended_full, source * width, width, axis=1)
        for source, unused in blocks
    ]
    weight = jnp.concatenate([block for unused, block in blocks], axis=0)
    return jnp.dot(jnp.concatenate(pieces, axis=1), weight, preferred_element_type=jnp.float32)


def on_device(
    section_input,
    row_code,
    code_table,
    self_gain,
    self_weights,
    self_out,
    cross_gain,
    memory_gain,
    cross_weights,
    cross_out,
):
    local_rows = section_input.shape[1]
    local_width = section_input.shape[2]
    codes_total = code_table.shape[1]
    me = lax.axis_index(MP)
    self_other, self_near = spread_rows(self_out[0])
    cross_blocks = spread(
        lambda target: lax.dynamic_slice_in_dim(cross_out, target * local_width, local_width, axis=1)
    )
    matches = (
        row_code[0][:, None] == lax.broadcasted_iota(jnp.int32, (local_rows, codes_total), 1)
    ).astype(jnp.bfloat16)
    looked = jnp.dot(matches, code_table[0], preferred_element_type=jnp.float32)
    embedded = (section_input[0].astype(jnp.float32) + looked).astype(jnp.bfloat16)
    embedded_full = lax.all_gather(embedded, MP, axis=1, tiled=True)
    normed = rms_norm(embedded_full, self_gain[0])
    self_queries = project(normed, self_weights[0, 0])
    self_pairs = jnp.stack(
        [project(normed, self_weights[0, 1]), project(normed, self_weights[0, 2])]
    )
    self_local, (self_other, self_near, cross_blocks) = attend(
        self_queries, self_pairs, (self_other, self_near, cross_blocks), by_permutes=True
    )
    self_blocks = rows_in_order(self_out[0], self_other, self_near)
    self_attended = lax.all_gather(self_local, MP, axis=1, tiled=True)
    hidden_full = (
        embedded_full.astype(jnp.float32) + project_out(self_attended, self_blocks)
    ).astype(jnp.bfloat16)
    hidden_part = lax.dynamic_slice_in_dim(hidden_full, me * local_width, local_width, axis=1)
    cross_queries = project(rms_norm(hidden_full, cross_gain), cross_weights[0])
    memory_normed = rms_norm(hidden_full, memory_gain)
    memory_pairs = jnp.stack(
        [project(memory_normed, cross_weights[1]), project(memory_normed, cross_weights[2])]
    )
    voxel_queries = shifted(cross_queries, "segment", -1)
    voxel_part = shifted(hidden_part, "segment", -1)
    crossed = mp_gather_flat(attend(voxel_queries, memory_pairs, by_permutes=True))
    decoded = (
        voxel_part.astype(jnp.float32) + project_out(crossed, cross_blocks)
    ).astype(jnp.bfloat16)
    returned = shifted(decoded, "segment", 1)
    chosen = jnp.where(lax.axis_index("segment") == 0, hidden_part, returned)
    return chosen[None]


def solution(mesh):
    segments, blocks, parts = (mesh.shape["segment"], mesh.shape["blk"], mesh.shape["mp"])
    split = Mesh(
        mesh.devices.reshape(segments, blocks // X_SIZE, X_SIZE, parts // CORES, CORES),
        ("segment", "bz", "bx", "my", "mc"),
    )
    rows = ("bz", "bx")
    return jax.shard_map(
        on_device,
        mesh=split,
        in_specs=(
            P("segment", rows, MP),
            P("segment", rows),
            P("segment", None, MP),
            P("segment", None),
            P("segment", None, None, MP),
            P("segment", MP, None),
            P(),
            P(),
            P(None, None, MP),
            P(MP, None),
        ),
        out_specs=P("segment", rows, MP),
        check_vma=False,
    )
```

```python
import math

import jax
import jax.numpy as jnp
from jax import lax
from jax.experimental import pallas as pl
from jax.experimental.pallas import tpu as pltpu
from jax.sharding import Mesh
from jax.sharding import PartitionSpec as P

HEAD_DIM = 128
MP = ("my", "mc")
X_SIZE = 4
CORES = 2
TILE = 256
STATS = 128
PARTS = 3


def shifted(value, axis, steps):
    count = lax.axis_size(axis)
    initial, last = (max(0, -steps), min(count, count - steps))
    return lax.ppermute(value, axis, [(source, source + steps) for source in range(initial, last)])


def rms_norm(values, gain):
    widened = values.astype(jnp.float32)
    meansq = jnp.mean(widened * widened, axis=-1, keepdims=True)
    return (widened * lax.rsqrt(meansq + 1e-05) * gain).astype(jnp.bfloat16)


def project(normed, weight):
    return jnp.dot(normed, weight, preferred_element_type=jnp.float32).astype(jnp.bfloat16)


def split_parts(value, count):
    parts = []
    rest = value
    for unused in range(count):
        part = rest.astype(jnp.bfloat16).astype(jnp.float32)
        parts.append(part)
        rest = rest - part
    return parts


def partial_kernel(q_ref, k_ref, v_ref, o_ref):
    heads = q_ref.shape[1] // HEAD_DIM
    rows = q_ref.shape[0]
    lane = lax.broadcasted_iota(jnp.int32, (rows, STATS), 1)
    stats = jnp.zeros((rows, STATS), jnp.float32)
    for h in range(heads):
        cols = slice(h * HEAD_DIM, (h + 1) * HEAD_DIM)
        scores = lax.dot_general(
            q_ref[:, cols], k_ref[:, cols], (((1,), (1,)), ((), ())),
            preferred_element_type=jnp.float32,
        )
        largest = jnp.max(scores, axis=1, keepdims=True)
        weights = jnp.exp2((scores - largest) * (math.log2(math.e) / math.sqrt(HEAD_DIM)))
        summed = jnp.sum(weights, axis=1, keepdims=True)
        largest = largest * (1.0 / math.sqrt(HEAD_DIM))
        o_ref[:, cols] = jnp.dot(
            weights.astype(jnp.bfloat16), v_ref[:, cols], preferred_element_type=jnp.float32
        ).astype(o_ref.dtype)
        for kind, value in enumerate((largest, summed)):
            for piece, part in enumerate(split_parts(value, PARTS)):
                slot = (kind * heads + h) * PARTS + piece
                stats = jnp.where(lane == slot, part, stats)
    o_ref[:, heads * HEAD_DIM:] = stats.astype(o_ref.dtype)


def partial_attend(queries, pairs):
    rows, width = queries.shape
    keys = pairs.shape[1]
    return pl.pallas_call(
        partial_kernel,
        grid=(rows // TILE,),
        in_specs=[
            pl.BlockSpec((TILE, width), lambda i: (i, 0)),
            pl.BlockSpec((None, keys, width), lambda i: (0, 0, 0)),
            pl.BlockSpec((None, keys, width), lambda i: (1, 0, 0)),
        ],
        out_specs=pl.BlockSpec((TILE, width + STATS), lambda i: (i, 0)),
        out_shape=jax.ShapeDtypeStruct((rows, width + STATS), jnp.bfloat16),
        compiler_params=pltpu.CompilerParams(vmem_limit_bytes=48 * 1024 * 1024),
    )(queries, pairs, pairs)


def attend(queries, pairs, riders=None, by_permutes=False):
    rows, width = queries.shape
    heads = width // HEAD_DIM
    query_block = lax.all_gather(queries, "bx", axis=0, tiled=True)
    key_block = lax.all_gather(pairs, "bz", axis=1, tiled=True)
    partial = partial_attend(query_block, key_block)
    if riders is not None:
        partial, riders = lax.optimization_barrier((partial, riders))
    if by_permutes:
        count = lax.axis_size("bx")
        me = lax.axis_index("bx")
        chunks = [lax.dynamic_slice_in_dim(partial, me * rows, rows, axis=0)]
        for step in range(1, count):
            piece = lax.dynamic_slice_in_dim(partial, ((me + step) % count) * rows, rows, axis=0)
            chunks.append(
                lax.ppermute(piece, "bx", [(j, (j + step) % count) for j in range(count)])
            )
        parts = jnp.stack(chunks)
    else:
        parts = lax.all_to_all(partial, "bx", 0, 0, tiled=True)
    parts = parts.reshape(-1, rows, width + STATS).astype(jnp.float32)
    outs = parts[:, :, :width].reshape(-1, rows, heads, HEAD_DIM)
    stats = parts[:, :, width:width + 2 * heads * PARTS].reshape(-1, rows, 2, heads, PARTS)
    stats = jnp.sum(stats, axis=-1)
    maxes = stats[:, :, 0]
    sums = stats[:, :, 1]
    top = jnp.max(maxes, axis=0)
    scale = jnp.exp(maxes - top[None])
    total = jnp.sum(sums * scale, axis=0)
    merged = jnp.sum(outs * scale[..., None], axis=0) / total[..., None]
    merged = merged.reshape(rows, width).astype(jnp.bfloat16)
    return merged if riders is None else (merged, riders)


def spread(block_of):
    count = lax.axis_size(MP)
    me = lax.axis_index(MP)
    blocks = [(me, block_of(me))]
    for step in range(1, count):
        piece = block_of((me + step) % count)
        received = lax.ppermute(piece, MP, [(j, (j + step) % count) for j in range(count)])
        blocks.append(((me - step + count) % count, received))
    return blocks


def spread_rows(block):
    other = lax.ppermute(block, "my", [(0, 1), (1, 0)])
    near = lax.ppermute(block, "mc", [(0, 1), (1, 0)])
    return other, near


def rows_in_order(block, other, near):
    my, mc = lax.axis_index("my"), lax.axis_index("mc")
    cores = lax.axis_size("mc")
    far = lax.ppermute(other, "mc", [(0, 1), (1, 0)])
    return [
        (my * cores + mc, block),
        ((1 - my) * cores + mc, other),
        (my * cores + 1 - mc, near),
        ((1 - my) * cores + 1 - mc, far),
    ]


def mp_gather_flat(value):
    return lax.all_gather(value, MP, axis=1, tiled=True)


def project_out(attended_full, blocks):
    width = blocks[0][1].shape[0]
    pieces = [
        lax.dynamic_slice_in_dim(attended_full, source * width, width, axis=1)
        for source, unused in blocks
    ]
    weight = jnp.concatenate([block for unused, block in blocks], axis=0)
    return jnp.dot(jnp.concatenate(pieces, axis=1), weight, preferred_element_type=jnp.float32)


def on_device(
    section_input,
    row_code,
    code_table,
    self_gain,
    self_weights,
    self_out,
    cross_gain,
    memory_gain,
    cross_weights,
    cross_out,
):
    local_rows = section_input.shape[1]
    local_width = section_input.shape[2]
    codes_total = code_table.shape[1]
    me = lax.axis_index(MP)
    self_other, self_near = spread_rows(self_out[0])
    cross_blocks = spread(
        lambda target: lax.dynamic_slice_in_dim(cross_out, target * local_width, local_width, axis=1)
    )
    matches = (
        row_code[0][:, None] == lax.broadcasted_iota(jnp.int32, (local_rows, codes_total), 1)
    ).astype(jnp.bfloat16)
    looked = jnp.dot(matches, code_table[0], preferred_element_type=jnp.float32)
    embedded = (section_input[0].astype(jnp.float32) + looked).astype(jnp.bfloat16)
    embedded_full = lax.all_gather(embedded, MP, axis=1, tiled=True)
    normed = rms_norm(embedded_full, self_gain[0])
    self_queries = project(normed, self_weights[0, 0])
    self_pairs = jnp.stack(
        [project(normed, self_weights[0, 1]), project(normed, self_weights[0, 2])]
    )
    self_local, (self_other, self_near, cross_blocks) = attend(
        self_queries, self_pairs, (self_other, self_near, cross_blocks), by_permutes=True
    )
    self_blocks = rows_in_order(self_out[0], self_other, self_near)
    self_attended = lax.all_gather(self_local, MP, axis=1, tiled=True)
    hidden_full = (
        embedded_full.astype(jnp.float32) + project_out(self_attended, self_blocks)
    ).astype(jnp.bfloat16)
    hidden_part = lax.dynamic_slice_in_dim(hidden_full, me * local_width, local_width, axis=1)
    cross_queries = project(rms_norm(hidden_full, cross_gain), cross_weights[0])
    memory_normed = rms_norm(hidden_full, memory_gain)
    memory_pairs = jnp.stack(
        [project(memory_normed, cross_weights[1]), project(memory_normed, cross_weights[2])]
    )
    voxel_queries, voxel_part = shifted(jnp.stack([cross_queries, hidden_part]), "segment", -1)
    crossed = mp_gather_flat(attend(voxel_queries, memory_pairs))
    decoded = (
        voxel_part.astype(jnp.float32) + project_out(crossed, cross_blocks)
    ).astype(jnp.bfloat16)
    returned = shifted(decoded, "segment", 1)
    chosen = jnp.where(lax.axis_index("segment") == 0, hidden_part, returned)
    return chosen[None]


def solution(mesh):
    segments, blocks, parts = (mesh.shape["segment"], mesh.shape["blk"], mesh.shape["mp"])
    split = Mesh(
        mesh.devices.reshape(segments, blocks // X_SIZE, X_SIZE, parts // CORES, CORES),
        ("segment", "bz", "bx", "my", "mc"),
    )
    rows = ("bz", "bx")
    return jax.shard_map(
        on_device,
        mesh=split,
        in_specs=(
            P("segment", rows, MP),
            P("segment", rows),
            P("segment", None, MP),
            P("segment", None),
            P("segment", None, None, MP),
            P("segment", MP, None),
            P(),
            P(),
            P(None, None, MP),
            P(MP, None),
        ),
        out_specs=P("segment", rows, MP),
        check_vma=False,
    )
```
